128 devices in a mesh: depth: 4 (over z), phi: 32 (over y, x, core).
Axes of the slice: x: 4, y: 4, z: 4, core: 2. Of those that a mesh axis runs over, the one named last changes fastest.
Arguments:
- grad_out: bfloat16 [448, 128, 32, 128], P('depth', 'phi'), may hold values from -6 to 6
- pre_act: bfloat16 [448, 128, 32, 128], P('depth', 'phi'), may hold values from -8 to 8
- w_first: bfloat16 [3, 3, 3, 32, 32], replicated, may hold values from -0.21875 to 0.21875
- w_second: bfloat16 [3, 3, 3, 32, 32], replicated, may hold values from -0.21875 to 0.21875
- map_blocks: bfloat16 [16384, 128, 128], P(('depth', 'phi')), may hold values from -0.15625 to 0.15625
- row_block: int32 [16384], P(('depth', 'phi')), may hold values from 0 to 447
- owner: int32 [16384, 1], P(('depth', 'phi')), may hold values from 0 to 127; in each aligned block of 128 rows (0 to 127, 128 to 255, ...) at most 2 rows name the same one
- col_local: int32 [16384], P(('depth', 'phi')), may hold values from 0 to 11
Outputs:
- cell_grad: float32 [1536, 32, 128], P(('depth', 'phi'))
The draws below stay inside these ranges and needn't reach their ends.
Inputs may be any that keep to these rules, and one draw needn't show every extreme that they name: Among the 128 blocks of one device no owner is named more than 2 times, and in some devices one owner is named exactly 2 times; every owner is named by some block.
All inputs are finite; a program needn't handle non-finite values.
Results may differ from the reference program's by a relative error of at most 0.0033.
Values may be sent and summed in bfloat16 or wider, within the bound.
No kernel may reach another device: no remote copies, remote signals or barrier semaphores. Data moves between devices by JAX's collectives and lax.ppermute only.
A program may use at most 192 MiB of HBM per device.

```python
import math
import jax
import jax.numpy as jnp
import numpy as np
from jax import lax

C = 32
E = 128
CBS = 128
PD = 4
DZ = 112
NB_DEV = 128
CB_DEV = 12
NZ = 448
NPHI = 128
OWNERS = 128
CAP = 2
BLOCKS = 16384
CELL_BLOCKS = 1536
RB_DEV = 448
N_DEPTH = 4
N_PHI = 32


def touch_ends(array, own_key, smallest, top_value):
    place = [jax.random.randint(jax.random.fold_in(own_key, axis), (), 0, length) for axis, length in enumerate(array.shape)]
    main_axis = array.shape.index(max(array.shape))
    neighbour = place[:main_axis] + [(place[main_axis] + 1) % array.shape[main_axis]] + place[main_axis + 1:]
    return array.at[tuple(place)].set(smallest).at[tuple(neighbour)].set(top_value)


def steps_of(key, dims, shards, low, high):
    gain = 1.0
    for axis_at, blocks in shards:
        draws = jax.random.uniform(jax.random.fold_in(jax.random.fold_in(key, 6), axis_at), (blocks,), jnp.float32, low / len(shards), high / len(shards))
        gain = gain * jnp.repeat(jnp.exp(draws), dims[axis_at] // blocks).reshape((-1,) + (1,) * (len(dims) - 1 - axis_at))
    return gain


def routed_block(own_key, own, number, rows, number_of, top, limit, slope):
    ranking = jax.random.permutation(own_key, number_of)
    packed, usual = portions_of(number_of, rows * top, limit, slope, True), portions_of(number_of, rows * top, limit, slope, False)
    places = jnp.arange(number_of)

    def named(sizes, rotation):
        used = int((sizes > 0).sum())
        fixed = max(1, used // 4)
        passed = fixed + (places - fixed + rotation * (used - fixed)) % max(1, number_of - fixed)
        return jnp.zeros((number_of,), jnp.int32).at[ranking[jnp.where(places < fixed, places, passed)]].set(jnp.asarray(sizes, jnp.int32))

    sizes = jnp.where(number % 4 == 0, named(packed, number // 4), named(usual, number - number // 4 - 1))
    mixed = jax.random.permutation(jax.random.fold_in(own, 3), number_of)
    giver, taker = mixed[0:number_of // 2 * 2:2], mixed[1:number_of // 2 * 2:2]
    room = jnp.minimum(sizes[giver] - 1, limit - sizes[taker]) // 2
    room = jnp.where((giver == ranking[0]) | (taker == ranking[0]) | (sizes[taker] == 0), 0, jnp.maximum(room, 0))
    passed = jax.random.randint(jax.random.fold_in(own, 4), (number_of // 2,), 0, 1 << 20) % (room + 1)
    sizes = sizes.at[giver].add(-passed).at[taker].add(passed)
    items = jnp.searchsorted(jnp.cumsum(sizes), jnp.arange(rows * top), side="right").astype(jnp.int32)
    grid = items.reshape(top, rows).T
    grid = grid[jax.random.permutation(jax.random.fold_in(own, 1), rows)]
    rotation = jax.random.randint(jax.random.fold_in(own, 2), (rows, 1), 0, top)
    return jnp.take_along_axis(grid, (jnp.arange(top)[None, :] + rotation) % top, axis=1)


def portions_of(amount, total, reach, lean, full):
    loads = [(1 << 20) // math.isqrt(standing ** lean) + 1 for standing in range(1, amount + 1)]
    largest = reach if full else min(reach, max(-(-total // amount), total * loads[0] // sum(loads)))
    least = 1 if total - largest >= amount - 1 else 0
    given, surplus = [largest] + [least] * (amount - 1), total - largest - least * (amount - 1)
    while surplus > 0:
        candidates = [i for i in range(1, amount) if given[i] < largest] or [i for i in range(1, amount) if given[i] < reach]
        whole, left = sum([loads[i] for i in candidates]), surplus
        for i in candidates:
            more = min(reach - given[i], max(1, left * loads[i] // whole), surplus)
            given[i] = given[i] + more
            surplus = surplus - more
    return np.array(given)


def bell_draw(own_key, dims, deviation, most, split=(), dtype=jnp.bfloat16):
    values = deviation * jax.random.normal(own_key, dims, jnp.float32)
    if split:
        values = values * steps_of(own_key, dims, split, -0.22, 0.18)
    return jnp.clip(values, -most, most).astype(dtype)


def setup_inputs(seed: int = 0) -> dict:
    seeds = jax.random.split(jax.random.key(seed), 9)
    grad_out = bell_draw(seeds[0], (NZ, NPHI, C, E), 1.0, 6.0, ((0, 4), (1, 32)))
    pre_act = bell_draw(seeds[1], (NZ, NPHI, C, E), 1.5, 8.0, ((0, 4), (1, 32)))
    w_first = bell_draw(seeds[2], (3, 3, 3, C, C), (27 * C) ** -0.5, 0.21875)
    w_second = bell_draw(seeds[3], (3, 3, 3, C, C), (27 * C) ** -0.5, 0.21875)
    map_blocks = bell_draw(seeds[4], (BLOCKS, E, CBS), (E * NB_DEV // CB_DEV) ** -0.5, 0.15625, ((0, 128),))
    row_block = touch_ends(jax.random.randint(seeds[5], (BLOCKS,), 0, RB_DEV), jax.random.fold_in(seeds[5], 1), 0, RB_DEV - 1).astype(jnp.int32)
    owner_keys = jax.random.split(jax.random.fold_in(seeds[6], 1), BLOCKS // NB_DEV)
    owner_turns = jax.random.permutation(jax.random.fold_in(seeds[6], 3), BLOCKS // NB_DEV)
    owner = jax.vmap(lambda own, number: routed_block(jax.random.fold_in(seeds[6], 2), own, number, NB_DEV, OWNERS, 1, CAP, 2))(owner_keys, owner_turns).reshape((BLOCKS, 1))
    col_local = touch_ends(jax.random.randint(seeds[7], (BLOCKS,), 0, CB_DEV), jax.random.fold_in(seeds[7], 1), 0, CB_DEV - 1).astype(jnp.int32)
    return dict(grad_out=grad_out, pre_act=pre_act, w_first=w_first, w_second=w_second, map_blocks=map_blocks, row_block=row_block, owner=owner, col_local=col_local)


def adjoint_conv(field, weight):
    wrapped = jnp.concatenate([field[:, -1:], field, field[:, :1]], axis=1)
    lhs = jnp.transpose(wrapped, (2, 0, 1, 3))[None].astype(jnp.float32)
    kernel = jnp.transpose(jnp.flip(weight, (0, 1, 2)), (3, 4, 0, 1, 2)).astype(jnp.float32)
    result = lax.conv_general_dilated(lhs, kernel, (1, 1, 1), ((1, 1), (0, 0), (1, 1)), dimension_numbers=("NCDHW", "OIDHW", "NCDHW"), precision=lax.Precision.HIGHEST)
    return jnp.transpose(result[0], (1, 2, 0, 3))


def reference(grad_out, pre_act, w_first, w_second, map_blocks, row_block, owner, col_local):
    back_second = adjoint_conv(grad_out, w_second)
    pre_val = pre_act.astype(jnp.float32)
    sigmoid_p = jax.nn.sigmoid(pre_val)
    hidden_grad = (back_second * sigmoid_p * (1.0 + pre_val * (1.0 - sigmoid_p))).astype(jnp.bfloat16)
    grid_grad = (adjoint_conv(hidden_grad, w_first) + grad_out.astype(jnp.float32)).astype(jnp.bfloat16)
    devices_all = N_DEPTH * N_PHI
    per_device = grid_grad.reshape(N_DEPTH, DZ, N_PHI, PD, C, E).transpose(0, 2, 1, 3, 4, 5).reshape(devices_all, DZ * PD, C, E)
    block_vals = map_blocks.reshape(devices_all, NB_DEV, E, CBS)
    row_ids = row_block.reshape(devices_all, NB_DEV).astype(jnp.int32)
    target = (owner[:, 0] * CB_DEV + col_local).reshape(devices_all, NB_DEV).astype(jnp.int32)

    def visit(summed, inputs):
        grid_rows, values, row_index, cell_index = inputs
        picked = grid_rows[row_index].astype(jnp.float32)
        partial_value = jnp.einsum("nce,nek->nck", picked, values.astype(jnp.float32), precision=lax.Precision.HIGHEST)
        return summed.at[cell_index].add(partial_value), None

    start = jnp.zeros((CELL_BLOCKS, C, CBS), jnp.float32)
    summed, unused = lax.scan(visit, start, (per_device, block_vals, row_ids, target))
    return summed
```

```python
import functools

import jax
import jax.numpy as jnp
from jax import lax
from jax.experimental import pallas as pl
from jax.experimental.pallas import tpu as pltpu
from jax.sharding import PartitionSpec as P

CB_DEV = 12
TZ = 8


def extended(block, sides, width, periodic):
    for axis, dim in sides:
        count = lax.axis_size(axis)
        forward = [(i, i + 1) for i in range(count - 1)]
        if periodic:
            forward.append((count - 1, 0))
        backward = [(target, source) for source, target in forward]
        low = lax.ppermute(
            lax.slice_in_dim(block, block.shape[dim] - width, None, axis=dim), axis, forward
        )
        high = lax.ppermute(lax.slice_in_dim(block, 0, width, axis=dim), axis, backward)
        block = jnp.concatenate([low, block, high], axis=dim)
    return block


def shifted(tile, c):
    if c == 0:
        return tile
    t = tile.astype(jnp.float32)
    e = t.shape[1]
    lane = lax.broadcasted_iota(jnp.int32, t.shape, 1)
    if c == 1:
        r = pltpu.roll(t, 1, 1)
        r = jnp.where(lane == 0, 0.0, r)
    else:
        r = pltpu.roll(t, e - 1, 1)
        r = jnp.where(lane == e - 1, 0.0, r)
    return r.astype(tile.dtype)


def conv_kernel(x_ref, w_ref, side_ref, o_ref, y_ref, *, tz, pd, ch, mode):
    step = pl.program_id(0)
    eta = x_ref.shape[3]

    def build(zin):
        for q in range(pd + 2):
            tile = x_ref[zin, q]
            for c in (-1, 0, 1):
                sh = shifted(tile, c)
                for p in range(pd):
                    b = p + 1 - q
                    if -1 <= b <= 1:
                        y_ref[zin, b + 1, pl.ds((c + 1) * ch, ch), pl.ds(p * eta, eta)] = sh

    @pl.when(step == 0)
    def _():
        build(0)
        build(1)

    def build_body(k, carry):
        build(step * tz + 2 + k)
        return carry

    lax.fori_loop(0, tz, build_body, 0)

    def body(zz, carry):
        z = step * tz + zz
        rhs = y_ref[pl.ds(z, 3)].reshape(9 * 3 * ch, pd * eta)
        acc = jnp.dot(w_ref[...], rhs, preferred_element_type=jnp.float32)
        for p in range(pd):
            part = acc[:, p * eta:(p + 1) * eta]
            side = side_ref[zz, p].astype(jnp.float32)
            if mode == "hidden":
                sig = jax.nn.sigmoid(side)
                val = part * sig * (1.0 + side * (1.0 - sig))
            else:
                val = part + side
            o_ref[zz, p] = val.astype(o_ref.dtype)
        return carry

    lax.fori_loop(0, tz, body, 0)


def conv_call(padded, weight, side, mode):
    zp, pp, ch, eta = padded.shape
    depth_len, pd = zp - 2, pp - 2
    wfull = jnp.transpose(jnp.flip(weight, 0), (3, 0, 1, 2, 4)).reshape(ch, 27 * ch)
    return pl.pallas_call(
        functools.partial(conv_kernel, tz=TZ, pd=pd, ch=ch, mode=mode),
        grid=(depth_len // TZ,),
        in_specs=[
            pl.BlockSpec((zp, pp, ch, eta), lambda i: (0, 0, 0, 0), pipeline_mode=pl.Buffered(1)),
            pl.BlockSpec((ch, 27 * ch), lambda i: (0, 0), pipeline_mode=pl.Buffered(1)),
            pl.BlockSpec((TZ, pd, ch, eta), lambda i: (i, 0, 0, 0)),
        ],
        out_specs=pl.BlockSpec((TZ, pd, ch, eta), lambda i: (i, 0, 0, 0)),
        out_shape=jax.ShapeDtypeStruct((depth_len, pd, ch, eta), jnp.bfloat16),
        scratch_shapes=[pltpu.VMEM((zp, 3, 3 * ch, pd * eta), jnp.bfloat16)],
        compiler_params=pltpu.CompilerParams(vmem_limit_bytes=60 * 1024 * 1024),
    )(padded, wfull, side)


def body(grad_out, pre_act, w_first, w_second, map_blocks, row_block, owner, col_local):
    grad_around = extended(grad_out, (("phi", 1),), 1, True)
    grad_padded = extended(grad_around, (("depth", 0),), 1, False)
    hidden_grad = conv_call(grad_padded, w_second, pre_act, "hidden")
    hidden_around = extended(hidden_grad, (("phi", 1),), 1, True)
    hidden_padded = extended(hidden_around, (("depth", 0),), 1, False)
    grid_grad = conv_call(hidden_padded, w_first, grad_out, "grid")
    channels = grid_grad.shape[2]
    eta_len = grid_grad.shape[3]
    block_count = map_blocks.shape[0]
    cell_size = map_blocks.shape[2]
    voxel_rows = grid_grad.reshape(grid_grad.shape[0] * grid_grad.shape[1], channels, eta_len)
    picked = voxel_rows[row_block]
    partial_value = jnp.einsum(
        "nce,nek->nck", picked, map_blocks, preferred_element_type=jnp.float32
    ).astype(jnp.bfloat16)
    depth_count = lax.axis_size("depth")
    phi_count = lax.axis_size("phi")
    owners = depth_count * phi_count
    slots = max(2, 2 * block_count // owners)
    owner_ids = owner[:, 0]
    onehot = (owner_ids[:, None] == jnp.arange(owners, dtype=jnp.int32)[None, :]).astype(jnp.int32)
    earlier = jnp.cumsum(onehot, axis=0) - onehot
    slot_index = jnp.sum(earlier * onehot, axis=1)
    position = owner_ids * slots + slot_index
    id_row = jnp.broadcast_to(
        (col_local + 1).astype(jnp.bfloat16)[:, None, None], (block_count, 1, cell_size)
    )
    payload = jnp.concatenate([partial_value, id_row], axis=1)
    placement = (
        position[None, :] == jnp.arange(owners * slots, dtype=jnp.int32)[:, None]
    ).astype(jnp.bfloat16)
    buffer = jnp.einsum(
        "sn,nck->sck", placement, payload, preferred_element_type=jnp.float32
    ).astype(jnp.bfloat16)
    received = lax.all_to_all(
        buffer.reshape(owners, slots, channels + 1, cell_size),
        ("depth", "phi"),
        split_axis=0,
        concat_axis=0,
        tiled=True,
    ).reshape(owners * slots, channels + 1, cell_size)
    got_cells = received[:, channels, 0].astype(jnp.int32)
    selector = (
        got_cells[None, :] == jnp.arange(1, CB_DEV + 1, dtype=jnp.int32)[:, None]
    ).astype(jnp.bfloat16)
    cell_grad = jnp.einsum(
        "ts,sck->tck", selector, received[:, :channels], preferred_element_type=jnp.float32
    )
    return cell_grad


def solution(mesh):
    return jax.shard_map(
        body,
        mesh=mesh,
        in_specs=(
            P("depth", "phi", None, None),
            P("depth", "phi", None, None),
            P(),
            P(),
            P(("depth", "phi"), None, None),
            P(("depth", "phi")),
            P(("depth", "phi"), None),
            P(("depth", "phi")),
        ),
        out_specs=P(("depth", "phi"), None, None),
        check_vma=False,
    )
```

```python
import functools

import jax
import jax.numpy as jnp
from jax import lax
from jax.experimental import pallas as pl
from jax.experimental.pallas import tpu as pltpu
from jax.sharding import PartitionSpec as P

CB_DEV = 12
TZ = 8


def extended(block, sides, width, periodic):
    for axis, dim in sides:
        count = lax.axis_size(axis)
        forward = [(i, i + 1) for i in range(count - 1)]
        if periodic:
            forward.append((count - 1, 0))
        backward = [(target, source) for source, target in forward]
        low = lax.ppermute(
            lax.slice_in_dim(block, block.shape[dim] - width, None, axis=dim), axis, forward
        )
        high = lax.ppermute(lax.slice_in_dim(block, 0, width, axis=dim), axis, backward)
        block = jnp.concatenate([low, block, high], axis=dim)
    return block


def shifted(tile, c):
    if c == 0:
        return tile
    t = tile.astype(jnp.float32)
    e = t.shape[1]
    lane = lax.broadcasted_iota(jnp.int32, t.shape, 1)
    if c == 1:
        r = pltpu.roll(t, 1, 1)
        r = jnp.where(lane == 0, 0.0, r)
    else:
        r = pltpu.roll(t, e - 1, 1)
        r = jnp.where(lane == e - 1, 0.0, r)
    return r.astype(tile.dtype)


def conv_kernel(x_ref, w_ref, side_ref, o_ref, y_ref, *, tz, pd, ch, mode):
    step = pl.program_id(0)
    eta = x_ref.shape[3]

    def build(zin):
        for q in range(pd + 2):
            tile = x_ref[zin, q]
            for c in (-1, 0, 1):
                sh = shifted(tile, c)
                for p in range(pd):
                    b = p + 1 - q
                    if -1 <= b <= 1:
                        y_ref[zin, b + 1, pl.ds((c + 1) * ch, ch), pl.ds(p * eta, eta)] = sh

    @pl.when(step == 0)
    def _():
        build(0)
        build(1)

    def build_body(k, carry):
        build(step * tz + 2 + k)
        return carry

    lax.fori_loop(0, tz, build_body, 0)

    def body(zz, carry):
        z = step * tz + zz
        rhs = y_ref[pl.ds(z, 3)].reshape(9 * 3 * ch, pd * eta)
        acc = jnp.dot(w_ref[...], rhs, preferred_element_type=jnp.float32)
        for p in range(pd):
            part = acc[:, p * eta:(p + 1) * eta]
            side = side_ref[zz, p].astype(jnp.float32)
            if mode == "hidden":
                sig = jax.nn.sigmoid(side)
                val = part * sig * (1.0 + side * (1.0 - sig))
            else:
                val = part + side
            o_ref[zz, p] = val.astype(o_ref.dtype)
        return carry

    lax.fori_loop(0, tz, body, 0)


def conv_call(padded, weight, side, mode):
    zp, pp, ch, eta = padded.shape
    depth_len, pd = zp - 2, pp - 2
    wfull = jnp.transpose(jnp.flip(weight, 0), (3, 0, 1, 2, 4)).reshape(ch, 27 * ch)
    return pl.pallas_call(
        functools.partial(conv_kernel, tz=TZ, pd=pd, ch=ch, mode=mode),
        grid=(depth_len // TZ,),
        in_specs=[
            pl.BlockSpec((zp, pp, ch, eta), lambda i: (0, 0, 0, 0), pipeline_mode=pl.Buffered(1)),
            pl.BlockSpec((ch, 27 * ch), lambda i: (0, 0), pipeline_mode=pl.Buffered(1)),
            pl.BlockSpec((TZ, pd, ch, eta), lambda i: (i, 0, 0, 0)),
        ],
        out_specs=pl.BlockSpec((TZ, pd, ch, eta), lambda i: (i, 0, 0, 0)),
        out_shape=jax.ShapeDtypeStruct((depth_len, pd, ch, eta), jnp.bfloat16),
        scratch_shapes=[pltpu.VMEM((zp, 3, 3 * ch, pd * eta), jnp.bfloat16)],
        compiler_params=pltpu.CompilerParams(vmem_limit_bytes=60 * 1024 * 1024),
    )(padded, wfull, side)


def map_kernel(rb_ref, pos_ref, cl_ref, hp_ref, w_ref, go_ref, mb_ref, zero_ref, o_ref, *, ch):
    del pos_ref, zero_ref
    n = pl.program_id(0)
    r = rb_ref[n]
    pd = hp_ref.shape[1] - 2
    z = r // pd
    p = r % pd
    pieces = []
    for j in range(3):
        for tap in range(3):
            tile = hp_ref[z + j, p + 2 - tap]
            for c in (-1, 0, 1):
                pieces.append(shifted(tile, c))
    rhs = jnp.concatenate(pieces, axis=0)
    acc = jnp.dot(w_ref[...], rhs, preferred_element_type=jnp.float32)
    row = (acc + go_ref[0, 0].astype(jnp.float32)).astype(jnp.bfloat16)
    part = jnp.dot(row, mb_ref[0], preferred_element_type=jnp.float32)
    o_ref[0, pl.ds(0, ch), :] = part.astype(o_ref.dtype)
    ids = jnp.full((1, o_ref.shape[2]), cl_ref[n] + 1, jnp.int32)
    o_ref[0, pl.ds(ch, 1), :] = ids.astype(jnp.float32).astype(o_ref.dtype)


def map_call(hidden_padded, weight, grad_out, map_blocks, row_block, position, col_local, slots_total):
    zp, pp, ch, eta = hidden_padded.shape
    pd = pp - 2
    block_count, _, cell_size = map_blocks.shape
    wfull = jnp.transpose(jnp.flip(weight, 0), (3, 0, 1, 2, 4)).reshape(ch, 27 * ch)
    zeros = jnp.zeros((slots_total, ch + 1, cell_size), jnp.bfloat16)
    grid_spec = pltpu.PrefetchScalarGridSpec(
        num_scalar_prefetch=3,
        grid=(block_count,),
        in_specs=[
            pl.BlockSpec((zp, pp, ch, eta), lambda n, rb, ps, cl: (0, 0, 0, 0),
                         pipeline_mode=pl.Buffered(1)),
            pl.BlockSpec((ch, 27 * ch), lambda n, rb, ps, cl: (0, 0), pipeline_mode=pl.Buffered(1)),
            pl.BlockSpec((1, 1, ch, eta), lambda n, rb, ps, cl: (rb[n] // pd, rb[n] % pd, 0, 0)),
            pl.BlockSpec((1, eta, cell_size), lambda n, rb, ps, cl: (n, 0, 0)),
            pl.BlockSpec(memory_space=pl.ANY),
        ],
        out_specs=pl.BlockSpec((1, ch + 1, cell_size), lambda n, rb, ps, cl: (ps[n], 0, 0)),
    )
    return pl.pallas_call(
        functools.partial(map_kernel, ch=ch),
        grid_spec=grid_spec,
        out_shape=jax.ShapeDtypeStruct((slots_total, ch + 1, cell_size), jnp.bfloat16),
        input_output_aliases={7: 0},
        compiler_params=pltpu.CompilerParams(vmem_limit_bytes=60 * 1024 * 1024),
    )(row_block, position, col_local, hidden_padded, wfull, grad_out, map_blocks, zeros)


def body(grad_out, pre_act, w_first, w_second, map_blocks, row_block, owner, col_local):
    grad_around = extended(grad_out, (("phi", 1),), 1, True)
    grad_padded = extended(grad_around, (("depth", 0),), 1, False)
    hidden_grad = conv_call(grad_padded, w_second, pre_act, "hidden")
    hidden_around = extended(hidden_grad, (("phi", 1),), 1, True)
    hidden_padded = extended(hidden_around, (("depth", 0),), 1, False)
    channels = grad_out.shape[2]
    block_count = map_blocks.shape[0]
    cell_size = map_blocks.shape[2]
    depth_count = lax.axis_size("depth")
    phi_count = lax.axis_size("phi")
    owners = depth_count * phi_count
    slots = max(2, 2 * block_count // owners)
    owner_ids = owner[:, 0]
    onehot = (owner_ids[:, None] == jnp.arange(owners, dtype=jnp.int32)[None, :]).astype(jnp.int32)
    earlier = jnp.cumsum(onehot, axis=0) - onehot
    slot_index = jnp.sum(earlier * onehot, axis=1)
    position = owner_ids * slots + slot_index
    buffer = map_call(
        hidden_padded, w_first, grad_out, map_blocks, row_block, position, col_local,
        owners * slots,
    )
    received = lax.all_to_all(
        buffer.reshape(owners, slots, channels + 1, cell_size),
        ("depth", "phi"),
        split_axis=0,
        concat_axis=0,
        tiled=True,
    ).reshape(owners * slots, channels + 1, cell_size)
    got_cells = received[:, channels, 0].astype(jnp.int32)
    selector = (
        got_cells[None, :] == jnp.arange(1, CB_DEV + 1, dtype=jnp.int32)[:, None]
    ).astype(jnp.bfloat16)
    cell_grad = jnp.einsum(
        "ts,sck->tck", selector, received[:, :channels], preferred_element_type=jnp.float32
    )
    return cell_grad


def solution(mesh):
    return jax.shard_map(
        body,
        mesh=mesh,
        in_specs=(
            P("depth", "phi", None, None),
            P("depth", "phi", None, None),
            P(),
            P(),
            P(("depth", "phi"), None, None),
            P(("depth", "phi")),
            P(("depth", "phi"), None),
            P(("depth", "phi")),
        ),
        out_specs=P(("depth", "phi"), None, None),
        check_vma=False,
    )
```

```python
import functools

import jax
import jax.numpy as jnp
from jax import lax
from jax.experimental import pallas as pl
from jax.experimental.pallas import tpu as pltpu
from jax.sharding import PartitionSpec as P

CB_DEV = 12
TZ = 8


def extended(block, sides, width, periodic):
    for axis, dim in sides:
        count = lax.axis_size(axis)
        forward = [(i, i + 1) for i in range(count - 1)]
        if periodic:
            forward.append((count - 1, 0))
        backward = [(target, source) for source, target in forward]
        low = lax.ppermute(
            lax.slice_in_dim(block, block.shape[dim] - width, None, axis=dim), axis, forward
        )
        high = lax.ppermute(lax.slice_in_dim(block, 0, width, axis=dim), axis, backward)
        block = jnp.concatenate([low, block, high], axis=dim)
    return block


def shifted(tile, c):
    if c == 0:
        return tile
    t = tile.astype(jnp.float32)
    e = t.shape[1]
    lane = lax.broadcasted_iota(jnp.int32, t.shape, 1)
    if c == 1:
        r = pltpu.roll(t, 1, 1)
        r = jnp.where(lane == 0, 0.0, r)
    else:
        r = pltpu.roll(t, e - 1, 1)
        r = jnp.where(lane == e - 1, 0.0, r)
    return r.astype(tile.dtype)


def conv_kernel(x_ref, w_ref, side_ref, o_ref, y_ref, *, tz, pd, ch, mode):
    step = pl.program_id(0)
    eta = x_ref.shape[3]

    def build(zin):
        for q in range(pd + 2):
            tile = x_ref[zin, q]
            for c in (-1, 0, 1):
                sh = shifted(tile, c)
                for p in range(pd):
                    b = p + 1 - q
                    if -1 <= b <= 1:
                        y_ref[zin, b + 1, pl.ds((c + 1) * ch, ch), pl.ds(p * eta, eta)] = sh

    @pl.when(step == 0)
    def _():
        build(0)
        build(1)

    def build_body(k, carry):
        build(step * tz + 2 + k)
        return carry

    lax.fori_loop(0, tz, build_body, 0)

    def body(zz, carry):
        z = step * tz + zz
        rhs = y_ref[pl.ds(z, 3)].reshape(9 * 3 * ch, pd * eta)
        acc = jnp.dot(w_ref[...], rhs, preferred_element_type=jnp.float32)
        for p in range(pd):
            part = acc[:, p * eta:(p + 1) * eta]
            side = side_ref[zz, p].astype(jnp.float32)
            if mode == "hidden":
                sig = jax.nn.sigmoid(side)
                val = part * sig * (1.0 + side * (1.0 - sig))
            else:
                val = part + side
            o_ref[zz, p] = val.astype(o_ref.dtype)
        return carry

    lax.fori_loop(0, tz, body, 0)


def conv_call(padded, weight, side, mode):
    zp, pp, ch, eta = padded.shape
    depth_len, pd = zp - 2, pp - 2
    wfull = jnp.transpose(jnp.flip(weight, 0), (3, 0, 1, 2, 4)).reshape(ch, 27 * ch)
    return pl.pallas_call(
        functools.partial(conv_kernel, tz=TZ, pd=pd, ch=ch, mode=mode),
        grid=(depth_len // TZ,),
        in_specs=[
            pl.BlockSpec((zp, pp, ch, eta), lambda i: (0, 0, 0, 0), pipeline_mode=pl.Buffered(1)),
            pl.BlockSpec((ch, 27 * ch), lambda i: (0, 0), pipeline_mode=pl.Buffered(1)),
            pl.BlockSpec((TZ, pd, ch, eta), lambda i: (i, 0, 0, 0)),
        ],
        out_specs=pl.BlockSpec((TZ, pd, ch, eta), lambda i: (i, 0, 0, 0)),
        out_shape=jax.ShapeDtypeStruct((depth_len, pd, ch, eta), jnp.bfloat16),
        scratch_shapes=[pltpu.VMEM((zp, 3, 3 * ch, pd * eta), jnp.bfloat16)],
        compiler_params=pltpu.CompilerParams(vmem_limit_bytes=60 * 1024 * 1024),
    )(padded, wfull, side)


def map_kernel(rb_ref, cl_ref, hp_ref, w_ref, go_ref, mb_ref, o_ref, *, ch, group):
    step = pl.program_id(0)
    pd = hp_ref.shape[1] - 2

    def one(g, carry):
        n = step * group + g
        r = rb_ref[n]
        z = r // pd
        p = r % pd
        pieces = []
        for j in range(3):
            for tap in range(3):
                tile = hp_ref[z + j, p + 2 - tap]
                for c in (-1, 0, 1):
                    pieces.append(shifted(tile, c))
        rhs = jnp.concatenate(pieces, axis=0)
        acc = jnp.dot(w_ref[...], rhs, preferred_element_type=jnp.float32)
        row = (acc + go_ref[z, p].astype(jnp.float32)).astype(jnp.bfloat16)
        part = jnp.dot(row, mb_ref[g], preferred_element_type=jnp.float32)
        o_ref[g, pl.ds(0, ch), :] = part.astype(o_ref.dtype)
        ids = jnp.full((1, o_ref.shape[2]), cl_ref[n] + 1, jnp.int32)
        o_ref[g, pl.ds(ch, 1), :] = ids.astype(jnp.float32).astype(o_ref.dtype)
        return carry

    lax.fori_loop(0, group, one, 0)


MAP_GROUP = 16


def map_call(hidden_padded, weight, grad_out, map_blocks, row_block, col_local):
    zp, pp, ch, eta = hidden_padded.shape
    block_count, _, cell_size = map_blocks.shape
    wfull = jnp.transpose(jnp.flip(weight, 0), (3, 0, 1, 2, 4)).reshape(ch, 27 * ch)
    grid_spec = pltpu.PrefetchScalarGridSpec(
        num_scalar_prefetch=2,
        grid=(block_count // MAP_GROUP,),
        in_specs=[
            pl.BlockSpec((zp, pp, ch, eta), lambda i, rb, cl: (0, 0, 0, 0),
                         pipeline_mode=pl.Buffered(1)),
            pl.BlockSpec((ch, 27 * ch), lambda i, rb, cl: (0, 0), pipeline_mode=pl.Buffered(1)),
            pl.BlockSpec(grad_out.shape, lambda i, rb, cl: (0, 0, 0, 0),
                         pipeline_mode=pl.Buffered(1)),
            pl.BlockSpec((MAP_GROUP, eta, cell_size), lambda i, rb, cl: (i, 0, 0)),
        ],
        out_specs=pl.BlockSpec((MAP_GROUP, ch + 1, cell_size), lambda i, rb, cl: (i, 0, 0)),
    )
    return pl.pallas_call(
        functools.partial(map_kernel, ch=ch, group=MAP_GROUP),
        grid_spec=grid_spec,
        out_shape=jax.ShapeDtypeStruct((block_count, ch + 1, cell_size), jnp.bfloat16),
        compiler_params=pltpu.CompilerParams(vmem_limit_bytes=60 * 1024 * 1024),
    )(row_block, col_local, hidden_padded, wfull, grad_out, map_blocks)


def body(grad_out, pre_act, w_first, w_second, map_blocks, row_block, owner, col_local):
    grad_around = extended(grad_out, (("phi", 1),), 1, True)
    grad_padded = extended(grad_around, (("depth", 0),), 1, False)
    hidden_grad = conv_call(grad_padded, w_second, pre_act, "hidden")
    hidden_around = extended(hidden_grad, (("phi", 1),), 1, True)
    hidden_padded = extended(hidden_around, (("depth", 0),), 1, False)
    channels = grad_out.shape[2]
    block_count = map_blocks.shape[0]
    cell_size = map_blocks.shape[2]
    depth_count = lax.axis_size("depth")
    phi_count = lax.axis_size("phi")
    owners = depth_count * phi_count
    slots = max(2, 2 * block_count // owners)
    owner_ids = owner[:, 0]
    onehot = (owner_ids[:, None] == jnp.arange(owners, dtype=jnp.int32)[None, :]).astype(jnp.int32)
    earlier = jnp.cumsum(onehot, axis=0) - onehot
    slot_index = jnp.sum(earlier * onehot, axis=1)
    payload = map_call(hidden_padded, w_first, grad_out, map_blocks, row_block, col_local)
    placement = (
        (owner_ids[None, None, :] == jnp.arange(owners, dtype=jnp.int32)[:, None, None])
        & (slot_index[None, None, :] == jnp.arange(slots, dtype=jnp.int32)[None, :, None])
    ).astype(jnp.bfloat16)
    buffer = jnp.einsum(
        "osn,nck->ocsk", placement, payload, preferred_element_type=jnp.float32
    ).astype(jnp.bfloat16)
    received = lax.all_to_all(buffer, ("depth", "phi"), split_axis=0, concat_axis=0, tiled=True)
    got_cells = received[:, channels, :, 0].astype(jnp.int32)
    selector = (
        got_cells[None, :, :] == jnp.arange(1, CB_DEV + 1, dtype=jnp.int32)[:, None, None]
    ).astype(jnp.bfloat16)
    cell_grad = jnp.einsum(
        "tsx,scxk->tck", selector, received[:, :channels], preferred_element_type=jnp.float32
    )
    return cell_grad


def solution(mesh):
    return jax.shard_map(
        body,
        mesh=mesh,
        in_specs=(
            P("depth", "phi", None, None),
            P("depth", "phi", None, None),
            P(),
            P(),
            P(("depth", "phi"), None, None),
            P(("depth", "phi")),
            P(("depth", "phi"), None),
            P(("depth", "phi")),
        ),
        out_specs=P(("depth", "phi"), None, None),
        check_vma=False,
    )
```

```python
import functools

import jax
import jax.numpy as jnp
from jax import lax
from jax.experimental import pallas as pl
from jax.experimental.pallas import tpu as pltpu
from jax.sharding import PartitionSpec as P

CB_DEV = 12
TZ = 8


def extended(block, sides, width, periodic):
    for axis, dim in sides:
        count = lax.axis_size(axis)
        forward = [(i, i + 1) for i in range(count - 1)]
        if periodic:
            forward.append((count - 1, 0))
        backward = [(target, source) for source, target in forward]
        low = lax.ppermute(
            lax.slice_in_dim(block, block.shape[dim] - width, None, axis=dim), axis, forward
        )
        high = lax.ppermute(lax.slice_in_dim(block, 0, width, axis=dim), axis, backward)
        block = jnp.concatenate([low, block, high], axis=dim)
    return block


def shifted(tile, c):
    if c == 0:
        return tile
    t = tile.astype(jnp.float32)
    e = t.shape[1]
    lane = lax.broadcasted_iota(jnp.int32, t.shape, 1)
    if c == 1:
        r = pltpu.roll(t, 1, 1)
        r = jnp.where(lane == 0, 0.0, r)
    else:
        r = pltpu.roll(t, e - 1, 1)
        r = jnp.where(lane == e - 1, 0.0, r)
    return r.astype(tile.dtype)


def conv_kernel(x_ref, w_ref, side_ref, o_ref, y_ref, *, tz, pd, ch, mode):
    step = pl.program_id(0)
    eta = x_ref.shape[3]

    def build(zin):
        for q in range(pd + 2):
            tile = x_ref[zin, q]
            for c in (-1, 0, 1):
                sh = shifted(tile, c)
                for p in range(pd):
                    b = p + 1 - q
                    if -1 <= b <= 1:
                        y_ref[zin, b + 1, pl.ds((c + 1) * ch, ch), pl.ds(p * eta, eta)] = sh

    @pl.when(step == 0)
    def _():
        build(0)
        build(1)

    def build_body(k, carry):
        build(step * tz + 2 + k)
        return carry

    lax.fori_loop(0, tz, build_body, 0)

    def body(zz, carry):
        z = step * tz + zz
        rhs = y_ref[pl.ds(z, 3)].reshape(9 * 3 * ch, pd * eta)
        acc = jnp.dot(w_ref[...], rhs, preferred_element_type=jnp.float32)
        for p in range(pd):
            part = acc[:, p * eta:(p + 1) * eta]
            side = side_ref[zz, p].astype(jnp.float32)
            if mode == "hidden":
                sig = jax.nn.sigmoid(side)
                val = part * sig * (1.0 + side * (1.0 - sig))
            else:
                val = part + side
            o_ref[zz, p] = val.astype(o_ref.dtype)
        return carry

    lax.fori_loop(0, tz, body, 0)


def conv_call(padded, weight, side, mode):
    zp, pp, ch, eta = padded.shape
    depth_len, pd = zp - 2, pp - 2
    wfull = jnp.transpose(jnp.flip(weight, 0), (3, 0, 1, 2, 4)).reshape(ch, 27 * ch)
    return pl.pallas_call(
        functools.partial(conv_kernel, tz=TZ, pd=pd, ch=ch, mode=mode),
        grid=(depth_len // TZ,),
        in_specs=[
            pl.BlockSpec((zp, pp, ch, eta), lambda i: (0, 0, 0, 0), pipeline_mode=pl.Buffered(1)),
            pl.BlockSpec((ch, 27 * ch), lambda i: (0, 0), pipeline_mode=pl.Buffered(1)),
            pl.BlockSpec((TZ, pd, ch, eta), lambda i: (i, 0, 0, 0)),
        ],
        out_specs=pl.BlockSpec((TZ, pd, ch, eta), lambda i: (i, 0, 0, 0)),
        out_shape=jax.ShapeDtypeStruct((depth_len, pd, ch, eta), jnp.bfloat16),
        scratch_shapes=[pltpu.VMEM((zp, 3, 3 * ch, pd * eta), jnp.bfloat16)],
        compiler_params=pltpu.CompilerParams(vmem_limit_bytes=60 * 1024 * 1024),
    )(padded, wfull, side)


def map_kernel(rb_ref, cl_ref, hp_ref, w_ref, go_ref, mb_ref, o_ref, y_ref, *, ch, group):
    step = pl.program_id(0)
    pd = hp_ref.shape[1] - 2

    @pl.when(step == 0)
    def _():
        def build(zin, carry):
            for q in range(pd + 2):
                tile = hp_ref[zin, q]
                for c in (-1, 0, 1):
                    sh = shifted(tile, c)
                    for p in range(pd):
                        tap = p + 2 - q
                        if 0 <= tap <= 2:
                            y_ref[zin, p, tap, pl.ds((c + 1) * ch, ch), :] = sh
            return carry

        lax.fori_loop(0, hp_ref.shape[0], build, 0)

    def one(g, carry):
        n = step * group + g
        r = rb_ref[n]
        z = r // pd
        p = r % pd
        rhs = y_ref[pl.ds(z, 3), p].reshape(27 * ch, y_ref.shape[4])
        acc = jnp.dot(w_ref[...], rhs, preferred_element_type=jnp.float32)
        row = (acc + go_ref[z, p].astype(jnp.float32)).astype(jnp.bfloat16)
        part = jnp.dot(row, mb_ref[g], preferred_element_type=jnp.float32)
        o_ref[g, pl.ds(0, ch), :] = part.astype(o_ref.dtype)
        ids = jnp.full((1, o_ref.shape[2]), cl_ref[n] + 1, jnp.int32)
        o_ref[g, pl.ds(ch, 1), :] = ids.astype(jnp.float32).astype(o_ref.dtype)
        return carry

    lax.fori_loop(0, group, one, 0)


MAP_GROUP = 16


def map_call(hidden_padded, weight, grad_out, map_blocks, row_block, col_local):
    zp, pp, ch, eta = hidden_padded.shape
    block_count, _, cell_size = map_blocks.shape
    wfull = jnp.transpose(jnp.flip(weight, 0), (3, 0, 1, 2, 4)).reshape(ch, 27 * ch)
    grid_spec = pltpu.PrefetchScalarGridSpec(
        num_scalar_prefetch=2,
        grid=(block_count // MAP_GROUP,),
        in_specs=[
            pl.BlockSpec((zp, pp, ch, eta), lambda i, rb, cl: (0, 0, 0, 0),
                         pipeline_mode=pl.Buffered(1)),
            pl.BlockSpec((ch, 27 * ch), lambda i, rb, cl: (0, 0), pipeline_mode=pl.Buffered(1)),
            pl.BlockSpec(grad_out.shape, lambda i, rb, cl: (0, 0, 0, 0),
                         pipeline_mode=pl.Buffered(1)),
            pl.BlockSpec((MAP_GROUP, eta, cell_size), lambda i, rb, cl: (i, 0, 0)),
        ],
        out_specs=pl.BlockSpec((MAP_GROUP, ch + 1, cell_size), lambda i, rb, cl: (i, 0, 0)),
        scratch_shapes=[pltpu.VMEM((zp, pp - 2, 3, 3 * ch, eta), jnp.bfloat16)],
    )
    return pl.pallas_call(
        functools.partial(map_kernel, ch=ch, group=MAP_GROUP),
        grid_spec=grid_spec,
        out_shape=jax.ShapeDtypeStruct((block_count, ch + 1, cell_size), jnp.bfloat16),
        compiler_params=pltpu.CompilerParams(vmem_limit_bytes=60 * 1024 * 1024),
    )(row_block, col_local, hidden_padded, wfull, grad_out, map_blocks)


def body(grad_out, pre_act, w_first, w_second, map_blocks, row_block, owner, col_local):
    grad_around = extended(grad_out, (("phi", 1),), 1, True)
    grad_padded = extended(grad_around, (("depth", 0),), 1, False)
    hidden_grad = conv_call(grad_padded, w_second, pre_act, "hidden")
    hidden_around = extended(hidden_grad, (("phi", 1),), 1, True)
    hidden_padded = extended(hidden_around, (("depth", 0),), 1, False)
    channels = grad_out.shape[2]
    block_count = map_blocks.shape[0]
    cell_size = map_blocks.shape[2]
    depth_count = lax.axis_size("depth")
    phi_count = lax.axis_size("phi")
    owners = depth_count * phi_count
    slots = max(2, 2 * block_count // owners)
    owner_ids = owner[:, 0]
    onehot = (owner_ids[:, None] == jnp.arange(owners, dtype=jnp.int32)[None, :]).astype(jnp.int32)
    earlier = jnp.cumsum(onehot, axis=0) - onehot
    slot_index = jnp.sum(earlier * onehot, axis=1)
    payload = map_call(hidden_padded, w_first, grad_out, map_blocks, row_block, col_local)
    placement = (
        (owner_ids[None, None, :] == jnp.arange(owners, dtype=jnp.int32)[:, None, None])
        & (slot_index[None, None, :] == jnp.arange(slots, dtype=jnp.int32)[None, :, None])
    ).astype(jnp.bfloat16)
    buffer = jnp.einsum(
        "osn,nck->ocsk", placement, payload, preferred_element_type=jnp.float32
    ).astype(jnp.bfloat16)
    received = lax.all_to_all(buffer, ("depth", "phi"), split_axis=0, concat_axis=0, tiled=True)
    got_cells = received[:, channels, :, 0].astype(jnp.int32)
    selector = (
        got_cells[None, :, :] == jnp.arange(1, CB_DEV + 1, dtype=jnp.int32)[:, None, None]
    ).astype(jnp.bfloat16)
    cell_grad = jnp.einsum(
        "tsx,scxk->tck", selector, received[:, :channels], preferred_element_type=jnp.float32
    )
    return cell_grad


def solution(mesh):
    return jax.shard_map(
        body,
        mesh=mesh,
        in_specs=(
            P("depth", "phi", None, None),
            P("depth", "phi", None, None),
            P(),
            P(),
            P(("depth", "phi"), None, None),
            P(("depth", "phi")),
            P(("depth", "phi"), None),
            P(("depth", "phi")),
        ),
        out_specs=P(("depth", "phi"), None, None),
        check_vma=False,
    )
```

```python
import functools

import jax
import jax.numpy as jnp
from jax import lax
from jax.experimental import pallas as pl
from jax.experimental.pallas import tpu as pltpu
from jax.sharding import PartitionSpec as P

CB_DEV = 12
TZ = 8


def extended(block, sides, width, periodic):
    for axis, dim in sides:
        count = lax.axis_size(axis)
        forward = [(i, i + 1) for i in range(count - 1)]
        if periodic:
            forward.append((count - 1, 0))
        backward = [(target, source) for source, target in forward]
        low = lax.ppermute(
            lax.slice_in_dim(block, block.shape[dim] - width, None, axis=dim), axis, forward
        )
        high = lax.ppermute(lax.slice_in_dim(block, 0, width, axis=dim), axis, backward)
        block = jnp.concatenate([low, block, high], axis=dim)
    return block


def shifted(tile, c):
    if c == 0:
        return tile
    t = tile.astype(jnp.float32)
    e = t.shape[1]
    lane = lax.broadcasted_iota(jnp.int32, t.shape, 1)
    if c == 1:
        r = pltpu.roll(t, 1, 1)
        r = jnp.where(lane == 0, 0.0, r)
    else:
        r = pltpu.roll(t, e - 1, 1)
        r = jnp.where(lane == e - 1, 0.0, r)
    return r.astype(tile.dtype)


def conv_kernel(x_ref, w_ref, side_ref, o_ref, y_ref, *, tz, ps, z0, off, ch, mode):
    step = pl.program_id(0)
    eta = x_ref.shape[3]
    cols = sorted({p + 1 - b for p in ps for b in (-1, 0, 1)})

    def build(r):
        zin = z0 + r - off
        for q in cols:
            tile = x_ref[zin, q - off]
            for c in (-1, 0, 1):
                sh = shifted(tile, c)
                for k, p in enumerate(ps):
                    b = p + 1 - q
                    if -1 <= b <= 1:
                        y_ref[r, b + 1, pl.ds((c + 1) * ch, ch), pl.ds(k * eta, eta)] = sh

    @pl.when(step == 0)
    def _():
        build(0)
        build(1)

    def build_body(k, carry):
        build(step * tz + 2 + k)
        return carry

    lax.fori_loop(0, tz, build_body, 0)

    def body(t, carry):
        r = step * tz + t
        rhs = y_ref[pl.ds(r, 3)].reshape(9 * 3 * ch, len(ps) * eta)
        acc = jnp.dot(w_ref[...], rhs, preferred_element_type=jnp.float32)
        for k, p in enumerate(ps):
            part = acc[:, k * eta:(k + 1) * eta]
            side = side_ref[z0 + r, p].astype(jnp.float32)
            if mode == "hidden":
                sig = jax.nn.sigmoid(side)
                val = part * sig * (1.0 + side * (1.0 - sig))
            else:
                val = part + side
            o_ref[t, k] = val.astype(o_ref.dtype)
        return carry

    lax.fori_loop(0, tz, body, 0)


def conv_part(field, off, wfull, side, mode, ps, z0, nz, tz):
    ch, eta = field.shape[2], field.shape[3]
    return pl.pallas_call(
        functools.partial(conv_kernel, tz=tz, ps=ps, z0=z0, off=off, ch=ch, mode=mode),
        grid=(nz // tz,),
        in_specs=[
            pl.BlockSpec(field.shape, lambda i: (0, 0, 0, 0), pipeline_mode=pl.Buffered(1)),
            pl.BlockSpec(wfull.shape, lambda i: (0, 0), pipeline_mode=pl.Buffered(1)),
            pl.BlockSpec(side.shape, lambda i: (0, 0, 0, 0), pipeline_mode=pl.Buffered(1)),
        ],
        out_specs=pl.BlockSpec((tz, len(ps), ch, eta), lambda i: (i, 0, 0, 0)),
        out_shape=jax.ShapeDtypeStruct((nz, len(ps), ch, eta), jnp.bfloat16),
        scratch_shapes=[pltpu.VMEM((nz + 2, 3, 3 * ch, len(ps) * eta), jnp.bfloat16)],
        compiler_params=pltpu.CompilerParams(vmem_limit_bytes=60 * 1024 * 1024),
        cost_estimate=pl.CostEstimate(
            flops=2 * nz * len(ps) * eta * ch * 27 * ch * 8,
            transcendentals=nz * len(ps) * ch * eta,
            bytes_accessed=2 * (field.size + side.size + 2 * nz * len(ps) * ch * eta),
        ),
    )(field, wfull, side)


def adjoint_conv(field, weight, side, mode):
    depth_len, pd, ch, eta = field.shape
    wfull = jnp.transpose(jnp.flip(weight, 0), (3, 0, 1, 2, 4)).reshape(ch, 27 * ch)
    inner = tuple(range(1, pd - 1))
    outer = (0, pd - 1)
    half = (depth_len - 2) // 2
    mids = [conv_part(field, 1, wfull, side, mode, inner, z, half, INNER_TZ)
            for z in (1, 1 + half)]
    around = extended(field, (("phi", 1),), 1, True)
    padded = extended(around, (("depth", 0),), 1, False)
    edge = conv_part(padded, 0, wfull, side, mode, outer, 0, depth_len, TZ)
    ends = [conv_part(padded, 0, wfull, side, mode, inner, z, 1, 1) for z in (0, depth_len - 1)]
    centre = jnp.concatenate([ends[0], *mids, ends[1]], axis=0)
    return jnp.concatenate([edge[:, :1], centre, edge[:, 1:]], axis=1)


INNER_TZ = 11


def body(grad_out, pre_act, w_first, w_second, map_blocks, row_block, owner, col_local):
    hidden_grad = adjoint_conv(grad_out, w_second, pre_act, "hidden")
    grid_grad = adjoint_conv(hidden_grad, w_first, grad_out, "grid")
    channels = grid_grad.shape[2]
    eta_len = grid_grad.shape[3]
    block_count = map_blocks.shape[0]
    cell_size = map_blocks.shape[2]
    voxel_rows = grid_grad.reshape(grid_grad.shape[0] * grid_grad.shape[1], channels, eta_len)
    picked = voxel_rows[row_block]
    partial_value = jnp.einsum(
        "nce,nek->nck", picked, map_blocks, preferred_element_type=jnp.float32
    ).astype(jnp.bfloat16)
    depth_count = lax.axis_size("depth")
    phi_count = lax.axis_size("phi")
    owners = depth_count * phi_count
    slots = max(2, 2 * block_count // owners)
    owner_ids = owner[:, 0]
    onehot = (owner_ids[:, None] == jnp.arange(owners, dtype=jnp.int32)[None, :]).astype(jnp.int32)
    earlier = jnp.cumsum(onehot, axis=0) - onehot
    slot_index = jnp.sum(earlier * onehot, axis=1)
    position = owner_ids * slots + slot_index
    id_row = jnp.broadcast_to(
        (col_local + 1).astype(jnp.bfloat16)[:, None, None], (block_count, 1, cell_size)
    )
    payload = jnp.concatenate([partial_value, id_row], axis=1)
    placement = (
        position[None, :] == jnp.arange(owners * slots, dtype=jnp.int32)[:, None]
    ).astype(jnp.bfloat16)
    buffer = jnp.einsum(
        "sn,nck->sck", placement, payload, preferred_element_type=jnp.float32
    ).astype(jnp.bfloat16)
    received = lax.all_to_all(
        buffer.reshape(owners, slots, channels + 1, cell_size),
        ("depth", "phi"),
        split_axis=0,
        concat_axis=0,
        tiled=True,
    ).reshape(owners * slots, channels + 1, cell_size)
    got_cells = received[:, channels, 0].astype(jnp.int32)
    selector = (
        got_cells[None, :] == jnp.arange(1, CB_DEV + 1, dtype=jnp.int32)[:, None]
    ).astype(jnp.bfloat16)
    cell_grad = jnp.einsum(
        "ts,sck->tck", selector, received[:, :channels], preferred_element_type=jnp.float32
    )
    return cell_grad


def solution(mesh):
    return jax.shard_map(
        body,
        mesh=mesh,
        in_specs=(
            P("depth", "phi", None, None),
            P("depth", "phi", None, None),
            P(),
            P(),
            P(("depth", "phi"), None, None),
            P(("depth", "phi")),
            P(("depth", "phi"), None),
            P(("depth", "phi")),
        ),
        out_specs=P(("depth", "phi"), None, None),
        check_vma=False,
    )
```

```python
import functools

import jax
import jax.numpy as jnp
from jax import lax
from jax.experimental import pallas as pl
from jax.experimental.pallas import tpu as pltpu
from jax.sharding import PartitionSpec as P

CB_DEV = 12
TZ = 8


def padded_field(block):
    nd = lax.axis_size("depth")
    nq = lax.axis_size("phi")

    def pairs(dd, dq):
        out = []
        for d in range(nd):
            if 0 <= d + dd < nd:
                for q in range(nq):
                    out.append((d * nq + q, (d + dd) * nq + (q + dq) % nq))
        return out

    both = ("depth", "phi")
    phi_fwd = [(q, (q + 1) % nq) for q in range(nq)]
    phi_bwd = [(t, s) for s, t in phi_fwd]
    dep_fwd = [(d, d + 1) for d in range(nd - 1)]
    dep_bwd = [(t, s) for s, t in dep_fwd]
    low_phi = lax.ppermute(block[:, -1:], "phi", phi_fwd)
    high_phi = lax.ppermute(block[:, :1], "phi", phi_bwd)
    low_dep = lax.ppermute(block[-1:], "depth", dep_fwd)
    high_dep = lax.ppermute(block[:1], "depth", dep_bwd)
    low_low = lax.ppermute(block[-1:, -1:], both, pairs(1, 1))
    low_high = lax.ppermute(block[-1:, :1], both, pairs(1, -1))
    high_low = lax.ppermute(block[:1, -1:], both, pairs(-1, 1))
    high_high = lax.ppermute(block[:1, :1], both, pairs(-1, -1))
    top = jnp.concatenate([low_low, low_dep, low_high], axis=1)
    middle = jnp.concatenate([low_phi, block, high_phi], axis=1)
    bottom = jnp.concatenate([high_low, high_dep, high_high], axis=1)
    return jnp.concatenate([top, middle, bottom], axis=0)


def shifted(tile, c):
    if c == 0:
        return tile
    t = tile.astype(jnp.float32)
    e = t.shape[1]
    lane = lax.broadcasted_iota(jnp.int32, t.shape, 1)
    if c == 1:
        r = pltpu.roll(t, 1, 1)
        r = jnp.where(lane == 0, 0.0, r)
    else:
        r = pltpu.roll(t, e - 1, 1)
        r = jnp.where(lane == e - 1, 0.0, r)
    return r.astype(tile.dtype)


def conv_kernel(x_ref, w_ref, side_ref, o_ref, y_ref, *, tz, pd, ch, mode):
    step = pl.program_id(0)
    eta = x_ref.shape[3]

    def build(zin):
        for q in range(pd + 2):
            tile = x_ref[zin, q]
            for c in (-1, 0, 1):
                sh = shifted(tile, c)
                for p in range(pd):
                    b = p + 1 - q
                    if -1 <= b <= 1:
                        y_ref[zin, b + 1, pl.ds((c + 1) * ch, ch), pl.ds(p * eta, eta)] = sh

    @pl.when(step == 0)
    def _():
        build(0)
        build(1)

    def build_body(k, carry):
        build(step * tz + 2 + k)
        return carry

    lax.fori_loop(0, tz, build_body, 0)

    def body(zz, carry):
        z = step * tz + zz
        rhs = y_ref[pl.ds(z, 3)].reshape(9 * 3 * ch, pd * eta)
        acc = jnp.dot(w_ref[...], rhs, preferred_element_type=jnp.float32)
        for p in range(pd):
            part = acc[:, p * eta:(p + 1) * eta]
            side = side_ref[zz, p].astype(jnp.float32)
            if mode == "hidden":
                sig = jax.nn.sigmoid(side)
                val = part * sig * (1.0 + side * (1.0 - sig))
            else:
                val = part + side
            o_ref[zz, p] = val.astype(o_ref.dtype)
        return carry

    lax.fori_loop(0, tz, body, 0)


def conv_call(padded, weight, side, mode):
    zp, pp, ch, eta = padded.shape
    depth_len, pd = zp - 2, pp - 2
    wfull = jnp.transpose(jnp.flip(weight, 0), (3, 0, 1, 2, 4)).reshape(ch, 27 * ch)
    return pl.pallas_call(
        functools.partial(conv_kernel, tz=TZ, pd=pd, ch=ch, mode=mode),
        grid=(depth_len // TZ,),
        in_specs=[
            pl.BlockSpec((zp, pp, ch, eta), lambda i: (0, 0, 0, 0), pipeline_mode=pl.Buffered(1)),
            pl.BlockSpec((ch, 27 * ch), lambda i: (0, 0), pipeline_mode=pl.Buffered(1)),
            pl.BlockSpec((TZ, pd, ch, eta), lambda i: (i, 0, 0, 0)),
        ],
        out_specs=pl.BlockSpec((TZ, pd, ch, eta), lambda i: (i, 0, 0, 0)),
        out_shape=jax.ShapeDtypeStruct((depth_len, pd, ch, eta), jnp.bfloat16),
        scratch_shapes=[pltpu.VMEM((zp, 3, 3 * ch, pd * eta), jnp.bfloat16)],
        compiler_params=pltpu.CompilerParams(vmem_limit_bytes=60 * 1024 * 1024),
    )(padded, wfull, side)


def body(grad_out, pre_act, w_first, w_second, map_blocks, row_block, owner, col_local):
    grad_padded = padded_field(grad_out)
    hidden_grad = conv_call(grad_padded, w_second, pre_act, "hidden")
    hidden_padded = padded_field(hidden_grad)
    grid_grad = conv_call(hidden_padded, w_first, grad_out, "grid")
    channels = grid_grad.shape[2]
    eta_len = grid_grad.shape[3]
    block_count = map_blocks.shape[0]
    cell_size = map_blocks.shape[2]
    voxel_rows = grid_grad.reshape(grid_grad.shape[0] * grid_grad.shape[1], channels, eta_len)
    picked = voxel_rows[row_block]
    partial_value = jnp.einsum(
        "nce,nek->nck", picked, map_blocks, preferred_element_type=jnp.float32
    ).astype(jnp.bfloat16)
    depth_count = lax.axis_size("depth")
    phi_count = lax.axis_size("phi")
    owners = depth_count * phi_count
    slots = max(2, 2 * block_count // owners)
    owner_ids = owner[:, 0]
    onehot = (owner_ids[:, None] == jnp.arange(owners, dtype=jnp.int32)[None, :]).astype(jnp.int32)
    earlier = jnp.cumsum(onehot, axis=0) - onehot
    slot_index = jnp.sum(earlier * onehot, axis=1)
    position = owner_ids * slots + slot_index
    id_row = jnp.broadcast_to(
        (col_local + 1).astype(jnp.bfloat16)[:, None, None], (block_count, 1, cell_size)
    )
    payload = jnp.concatenate([partial_value, id_row], axis=1)
    placement = (
        position[None, :] == jnp.arange(owners * slots, dtype=jnp.int32)[:, None]
    ).astype(jnp.bfloat16)
    buffer = jnp.einsum(
        "sn,nck->sck", placement, payload, preferred_element_type=jnp.float32
    ).astype(jnp.bfloat16)
    received = lax.all_to_all(
        buffer.reshape(owners, slots, channels + 1, cell_size),
        ("depth", "phi"),
        split_axis=0,
        concat_axis=0,
        tiled=True,
    ).reshape(owners * slots, channels + 1, cell_size)
    got_cells = received[:, channels, 0].astype(jnp.int32)
    selector = (
        got_cells[None, :] == jnp.arange(1, CB_DEV + 1, dtype=jnp.int32)[:, None]
    ).astype(jnp.bfloat16)
    cell_grad = jnp.einsum(
        "ts,sck->tck", selector, received[:, :channels], preferred_element_type=jnp.float32
    )
    return cell_grad


def solution(mesh):
    return jax.shard_map(
        body,
        mesh=mesh,
        in_specs=(
            P("depth", "phi", None, None),
            P("depth", "phi", None, None),
            P(),
            P(),
            P(("depth", "phi"), None, None),
            P(("depth", "phi")),
            P(("depth", "phi"), None),
            P(("depth", "phi")),
        ),
        out_specs=P(("depth", "phi"), None, None),
        check_vma=False,
    )
```

```python
import functools

import jax
import jax.numpy as jnp
from jax import lax
from jax.experimental import pallas as pl
from jax.experimental.pallas import tpu as pltpu
from jax.sharding import PartitionSpec as P

CB_DEV = 12
TZ = 8


def halo_pieces(block):
    nq = lax.axis_size("phi")
    nd = lax.axis_size("depth")
    phi_fwd = [(q, (q + 1) % nq) for q in range(nq)]
    phi_bwd = [(t, s) for s, t in phi_fwd]
    dep_fwd = [(d, d + 1) for d in range(nd - 1)]
    dep_bwd = [(t, s) for s, t in dep_fwd]
    low_phi = lax.ppermute(block[:, -1:], "phi", phi_fwd)
    high_phi = lax.ppermute(block[:, :1], "phi", phi_bwd)
    first = jnp.concatenate([low_phi[:1], block[:1], high_phi[:1]], axis=1)
    last = jnp.concatenate([low_phi[-1:], block[-1:], high_phi[-1:]], axis=1)
    top = lax.ppermute(last, "depth", dep_fwd)
    bottom = lax.ppermute(first, "depth", dep_bwd)
    return block, low_phi, high_phi, top, bottom


def shifted(tile, c):
    if c == 0:
        return tile
    t = tile.astype(jnp.float32)
    e = t.shape[1]
    lane = lax.broadcasted_iota(jnp.int32, t.shape, 1)
    if c == 1:
        r = pltpu.roll(t, 1, 1)
        r = jnp.where(lane == 0, 0.0, r)
    else:
        r = pltpu.roll(t, e - 1, 1)
        r = jnp.where(lane == e - 1, 0.0, r)
    return r.astype(tile.dtype)


def conv_kernel(x_ref, lo_ref, hi_ref, top_ref, bot_ref, w_ref, side_ref, o_ref, y_ref,
                *, tz, pd, ch, mode):
    step = pl.program_id(0)
    eta = x_ref.shape[3]
    last_row = x_ref.shape[0] + 1

    def store(zin, q, tile):
        for c in (-1, 0, 1):
            sh = shifted(tile, c)
            for p in range(pd):
                b = p + 1 - q
                if -1 <= b <= 1:
                    y_ref[zin, b + 1, pl.ds((c + 1) * ch, ch), pl.ds(p * eta, eta)] = sh

    def build_end(zin, row_ref):
        for q in range(pd + 2):
            store(zin, q, row_ref[0, q])

    def build(zin):
        for q in range(pd + 2):
            if q == 0:
                tile = lo_ref[zin - 1, 0]
            elif q == pd + 1:
                tile = hi_ref[zin - 1, 0]
            else:
                tile = x_ref[zin - 1, q - 1]
            store(zin, q, tile)

    @pl.when(step == 0)
    def _():
        build_end(0, top_ref)
        build(1)

    def build_body(k, carry):
        zin = step * tz + 2 + k

        @pl.when(zin < last_row)
        def _():
            build(zin)

        @pl.when(zin == last_row)
        def _():
            build_end(last_row, bot_ref)

        return carry

    lax.fori_loop(0, tz, build_body, 0)

    def body(zz, carry):
        z = step * tz + zz
        rhs = y_ref[pl.ds(z, 3)].reshape(9 * 3 * ch, pd * eta)
        acc = jnp.dot(w_ref[...], rhs, preferred_element_type=jnp.float32)
        for p in range(pd):
            part = acc[:, p * eta:(p + 1) * eta]
            side = side_ref[zz, p].astype(jnp.float32)
            if mode == "hidden":
                sig = jax.nn.sigmoid(side)
                val = part * sig * (1.0 + side * (1.0 - sig))
            else:
                val = part + side
            o_ref[zz, p] = val.astype(o_ref.dtype)
        return carry

    lax.fori_loop(0, tz, body, 0)


def conv_call(pieces, weight, side, mode):
    field, low, high, top, bottom = pieces
    depth_len, pd, ch, eta = field.shape
    zp = depth_len + 2
    wfull = jnp.transpose(jnp.flip(weight, 0), (3, 0, 1, 2, 4)).reshape(ch, 27 * ch)

    def whole(a):
        return pl.BlockSpec(a.shape, lambda i: (0,) * a.ndim, pipeline_mode=pl.Buffered(1))

    return pl.pallas_call(
        functools.partial(conv_kernel, tz=TZ, pd=pd, ch=ch, mode=mode),
        grid=(depth_len // TZ,),
        in_specs=[
            whole(field), whole(low), whole(high), whole(top), whole(bottom), whole(wfull),
            pl.BlockSpec((TZ, pd, ch, eta), lambda i: (i, 0, 0, 0)),
        ],
        out_specs=pl.BlockSpec((TZ, pd, ch, eta), lambda i: (i, 0, 0, 0)),
        out_shape=jax.ShapeDtypeStruct((depth_len, pd, ch, eta), jnp.bfloat16),
        scratch_shapes=[pltpu.VMEM((zp, 3, 3 * ch, pd * eta), jnp.bfloat16)],
        compiler_params=pltpu.CompilerParams(vmem_limit_bytes=60 * 1024 * 1024),
    )(field, low, high, top, bottom, wfull, side)


def body(grad_out, pre_act, w_first, w_second, map_blocks, row_block, owner, col_local):
    hidden_grad = conv_call(halo_pieces(grad_out), w_second, pre_act, "hidden")
    grid_grad = conv_call(halo_pieces(hidden_grad), w_first, grad_out, "grid")
    channels = grid_grad.shape[2]
    eta_len = grid_grad.shape[3]
    block_count = map_blocks.shape[0]
    cell_size = map_blocks.shape[2]
    voxel_rows = grid_grad.reshape(grid_grad.shape[0] * grid_grad.shape[1], channels, eta_len)
    picked = voxel_rows[row_block]
    partial_value = jnp.einsum(
        "nce,nek->nck", picked, map_blocks, preferred_element_type=jnp.float32
    ).astype(jnp.bfloat16)
    depth_count = lax.axis_size("depth")
    phi_count = lax.axis_size("phi")
    owners = depth_count * phi_count
    slots = max(2, 2 * block_count // owners)
    owner_ids = owner[:, 0]
    onehot = (owner_ids[:, None] == jnp.arange(owners, dtype=jnp.int32)[None, :]).astype(jnp.int32)
    earlier = jnp.cumsum(onehot, axis=0) - onehot
    slot_index = jnp.sum(earlier * onehot, axis=1)
    position = owner_ids * slots + slot_index
    id_row = jnp.broadcast_to(
        (col_local + 1).astype(jnp.bfloat16)[:, None, None], (block_count, 1, cell_size)
    )
    payload = jnp.concatenate([partial_value, id_row], axis=1)
    placement = (
        position[None, :] == jnp.arange(owners * slots, dtype=jnp.int32)[:, None]
    ).astype(jnp.bfloat16)
    buffer = jnp.einsum(
        "sn,nck->sck", placement, payload, preferred_element_type=jnp.float32
    ).astype(jnp.bfloat16)
    received = lax.all_to_all(
        buffer.reshape(owners, slots, channels + 1, cell_size),
        ("depth", "phi"),
        split_axis=0,
        concat_axis=0,
        tiled=True,
    ).reshape(owners * slots, channels + 1, cell_size)
    got_cells = received[:, channels, 0].astype(jnp.int32)
    selector = (
        got_cells[None, :] == jnp.arange(1, CB_DEV + 1, dtype=jnp.int32)[:, None]
    ).astype(jnp.bfloat16)
    cell_grad = jnp.einsum(
        "ts,sck->tck", selector, received[:, :channels], preferred_element_type=jnp.float32
    )
    return cell_grad


def solution(mesh):
    return jax.shard_map(
        body,
        mesh=mesh,
        in_specs=(
            P("depth", "phi", None, None),
            P("depth", "phi", None, None),
            P(),
            P(),
            P(("depth", "phi"), None, None),
            P(("depth", "phi")),
            P(("depth", "phi"), None),
            P(("depth", "phi")),
        ),
        out_specs=P(("depth", "phi"), None, None),
        check_vma=False,
    )
```

```python
import functools

import jax
import jax.numpy as jnp
from jax import lax
from jax.experimental import pallas as pl
from jax.experimental.pallas import tpu as pltpu
from jax.sharding import PartitionSpec as P

CB_DEV = 12
TZ = 8


def halo_pieces(block):
    nq = lax.axis_size("phi")
    nd = lax.axis_size("depth")
    phi_fwd = [(q, (q + 1) % nq) for q in range(nq)]
    phi_bwd = [(t, s) for s, t in phi_fwd]
    dep_fwd = [(d, d + 1) for d in range(nd - 1)]
    dep_bwd = [(t, s) for s, t in dep_fwd]
    low_phi = lax.ppermute(block[:, -1:], "phi", phi_fwd)
    high_phi = lax.ppermute(block[:, :1], "phi", phi_bwd)
    first = jnp.concatenate([low_phi[:1], block[:1], high_phi[:1]], axis=1)
    last = jnp.concatenate([low_phi[-1:], block[-1:], high_phi[-1:]], axis=1)
    top = lax.ppermute(last, "depth", dep_fwd)
    bottom = lax.ppermute(first, "depth", dep_bwd)
    return block, low_phi, high_phi, top, bottom


def shifted(tile, c):
    if c == 0:
        return tile
    t = tile.astype(jnp.float32)
    e = t.shape[1]
    lane = lax.broadcasted_iota(jnp.int32, t.shape, 1)
    if c == 1:
        r = pltpu.roll(t, 1, 1)
        r = jnp.where(lane == 0, 0.0, r)
    else:
        r = pltpu.roll(t, e - 1, 1)
        r = jnp.where(lane == e - 1, 0.0, r)
    return r.astype(tile.dtype)


def conv_kernel(x_ref, lo_ref, hi_ref, top_ref, bot_ref, w_ref, *rest, tz, pd, ch, mode):
    if mode == "raw":
        o_ref, y_ref = rest
    else:
        side_ref, o_ref, y_ref = rest
    step = pl.program_id(0)
    eta = x_ref.shape[3]
    last_row = x_ref.shape[0] + 1

    def store(zin, q, tile):
        for c in (-1, 0, 1):
            sh = shifted(tile, c)
            for p in range(pd):
                b = p + 1 - q
                if -1 <= b <= 1:
                    y_ref[zin, b + 1, pl.ds((c + 1) * ch, ch), pl.ds(p * eta, eta)] = sh

    def build_end(zin, row_ref):
        for q in range(pd + 2):
            store(zin, q, row_ref[0, q])

    def build(zin):
        for q in range(pd + 2):
            if q == 0:
                tile = lo_ref[zin - 1, 0]
            elif q == pd + 1:
                tile = hi_ref[zin - 1, 0]
            else:
                tile = x_ref[zin - 1, q - 1]
            store(zin, q, tile)

    @pl.when(step == 0)
    def _():
        build_end(0, top_ref)
        build(1)

    def build_body(k, carry):
        zin = step * tz + 2 + k

        @pl.when(zin < last_row)
        def _():
            build(zin)

        @pl.when(zin == last_row)
        def _():
            build_end(last_row, bot_ref)

        return carry

    lax.fori_loop(0, tz, build_body, 0)

    def body(zz, carry):
        z = step * tz + zz
        rhs = y_ref[pl.ds(z, 3)].reshape(9 * 3 * ch, pd * eta)
        acc = jnp.dot(w_ref[...], rhs, preferred_element_type=jnp.float32)
        for p in range(pd):
            part = acc[:, p * eta:(p + 1) * eta]
            if mode == "raw":
                o_ref[zz, p] = part
                continue
            side = side_ref[zz, p].astype(jnp.float32)
            if mode == "hidden":
                sig = jax.nn.sigmoid(side)
                val = part * sig * (1.0 + side * (1.0 - sig))
            else:
                val = part + side
            o_ref[zz, p] = val.astype(o_ref.dtype)
        return carry

    lax.fori_loop(0, tz, body, 0)


def conv_call(pieces, weight, side, mode):
    field, low, high, top, bottom = pieces
    depth_len, pd, ch, eta = field.shape
    zp = depth_len + 2
    wfull = jnp.transpose(jnp.flip(weight, 0), (3, 0, 1, 2, 4)).reshape(ch, 27 * ch)
    block = pl.BlockSpec((TZ, pd, ch, eta), lambda i: (i, 0, 0, 0))
    operands = [field, low, high, top, bottom, wfull]
    specs = [whole(a) for a in operands]
    if mode != "raw":
        operands.append(side)
        specs.append(block)
    out_dtype = jnp.float32 if mode == "raw" else jnp.bfloat16
    return pl.pallas_call(
        functools.partial(conv_kernel, tz=TZ, pd=pd, ch=ch, mode=mode),
        grid=(depth_len // TZ,),
        in_specs=specs,
        out_specs=block,
        out_shape=jax.ShapeDtypeStruct((depth_len, pd, ch, eta), out_dtype),
        scratch_shapes=[pltpu.VMEM((zp, 3, 3 * ch, pd * eta), jnp.bfloat16)],
        compiler_params=pltpu.CompilerParams(vmem_limit_bytes=60 * 1024 * 1024),
        cost_estimate=pl.CostEstimate(
            flops=2 * field.size * 27 * ch, transcendentals=0,
            bytes_accessed=2 * field.size * 4),
    )(*operands)


def whole(a):
    return pl.BlockSpec(a.shape, lambda i: (0,) * a.ndim, pipeline_mode=pl.Buffered(1))


def halo_kernel(acc_ref, lo_ref, hi_ref, top_ref, bot_ref, ws_ref, wt_ref, side_ref, o_ref,
                l3_ref, e_ref, *, tz, pd, ch, mode):
    step = pl.program_id(0)
    depth_len = lo_ref.shape[0]
    eta = lo_ref.shape[3]
    cols = (0, pd + 1)

    def put(s, zin, tile):
        for c in (-1, 0, 1):
            l3_ref[s, zin, pl.ds((c + 1) * ch, ch), :] = shifted(tile, c)

    @pl.when(step == 0)
    def _():
        for s in range(2):
            put(s, 0, top_ref[0, cols[s]])
            put(s, depth_len + 1, bot_ref[0, cols[s]])

        def fill(zin, carry):
            put(0, zin, lo_ref[zin - 1, 0])
            put(1, zin, hi_ref[zin - 1, 0])
            return carry

        lax.fori_loop(1, depth_len + 1, fill, 0)
        zero = jnp.zeros((ch, eta), top_ref.dtype)
        for k, row_ref in enumerate((top_ref, bot_ref)):
            for p in range(pd):
                pieces = []
                for tap in range(3):
                    q = p + 2 - tap
                    tile = row_ref[0, q] if 1 <= q <= pd else zero
                    for c in (-1, 0, 1):
                        pieces.append(shifted(tile, c))
                rhs = jnp.concatenate(pieces, axis=0)
                e_ref[k, p] = jnp.dot(wt_ref[k], rhs, preferred_element_type=jnp.float32)

    def body(zz, carry):
        z = step * tz + zz
        for p in range(pd):
            total = acc_ref[zz, p]
            for s, ps in enumerate((0, pd - 1)):
                if p == ps:
                    rhs = l3_ref[s, pl.ds(z, 3)].reshape(9 * ch, eta)
                    total = total + jnp.dot(ws_ref[s], rhs, preferred_element_type=jnp.float32)
            total = total + jnp.where(z == 0, e_ref[0, p], 0.0)
            total = total + jnp.where(z == depth_len - 1, e_ref[1, p], 0.0)
            side = side_ref[zz, p].astype(jnp.float32)
            if mode == "hidden":
                sig = jax.nn.sigmoid(side)
                val = total * sig * (1.0 + side * (1.0 - sig))
            else:
                val = total + side
            o_ref[zz, p] = val.astype(o_ref.dtype)
        return carry

    lax.fori_loop(0, tz, body, 0)


def halo_call(acc, pieces, weight, side, mode):
    field, low, high, top, bottom = pieces
    depth_len, pd, ch, eta = field.shape
    flipped = jnp.flip(weight, 0)
    ws = jnp.stack([
        jnp.transpose(flipped[:, bidx], (2, 0, 1, 3)).reshape(ch, 9 * ch) for bidx in (2, 0)
    ])
    wt = jnp.stack([
        jnp.transpose(weight[aidx], (2, 0, 1, 3)).reshape(ch, 9 * ch) for aidx in (2, 0)
    ])
    block = pl.BlockSpec((TZ, pd, ch, eta), lambda i: (i, 0, 0, 0))
    return pl.pallas_call(
        functools.partial(halo_kernel, tz=TZ, pd=pd, ch=ch, mode=mode),
        grid=(depth_len // TZ,),
        in_specs=[block, whole(low), whole(high), whole(top), whole(bottom), whole(ws),
                  whole(wt), block],
        out_specs=block,
        out_shape=jax.ShapeDtypeStruct((depth_len, pd, ch, eta), jnp.bfloat16),
        scratch_shapes=[pltpu.VMEM((2, depth_len + 2, 3 * ch, eta), jnp.bfloat16),
                        pltpu.VMEM((2, pd, ch, eta), jnp.float32)],
        compiler_params=pltpu.CompilerParams(vmem_limit_bytes=60 * 1024 * 1024),
        cost_estimate=pl.CostEstimate(
            flops=2 * 2 * depth_len * ch * eta * 9 * ch, transcendentals=field.size,
            bytes_accessed=field.size * 8),
    )(acc, low, high, top, bottom, ws, wt, side)


def adjoint_conv(field, weight, side, mode):
    nq = lax.axis_size("phi")
    nd = lax.axis_size("depth")
    phi_fwd = [(q, (q + 1) % nq) for q in range(nq)]
    phi_bwd = [(t, s) for s, t in phi_fwd]
    dep_fwd = [(d, d + 1) for d in range(nd - 1)]
    dep_bwd = [(t, s) for s, t in dep_fwd]
    low_phi = lax.ppermute(field[:, -1:], "phi", phi_fwd)
    high_phi = lax.ppermute(field[:, :1], "phi", phi_bwd)
    quiet = (field, jnp.zeros_like(low_phi), jnp.zeros_like(high_phi),
             jnp.zeros_like(field[:1, :1]).repeat(field.shape[1] + 2, axis=1),
             jnp.zeros_like(field[:1, :1]).repeat(field.shape[1] + 2, axis=1))
    acc = conv_call(quiet, weight, None, "raw")
    first = jnp.concatenate([low_phi[:1], field[:1], high_phi[:1]], axis=1)
    last = jnp.concatenate([low_phi[-1:], field[-1:], high_phi[-1:]], axis=1)
    first, last, acc = lax.optimization_barrier((first, last, acc))
    top = lax.ppermute(last, "depth", dep_fwd)
    bottom = lax.ppermute(first, "depth", dep_bwd)
    return halo_call(acc, (field, low_phi, high_phi, top, bottom), weight, side, mode)


def body(grad_out, pre_act, w_first, w_second, map_blocks, row_block, owner, col_local):
    hidden_grad = adjoint_conv(grad_out, w_second, pre_act, "hidden")
    grid_grad = adjoint_conv(hidden_grad, w_first, grad_out, "grid")
    channels = grid_grad.shape[2]
    eta_len = grid_grad.shape[3]
    block_count = map_blocks.shape[0]
    cell_size = map_blocks.shape[2]
    voxel_rows = grid_grad.reshape(grid_grad.shape[0] * grid_grad.shape[1], channels, eta_len)
    picked = voxel_rows[row_block]
    partial_value = jnp.einsum(
        "nce,nek->nck", picked, map_blocks, preferred_element_type=jnp.float32
    ).astype(jnp.bfloat16)
    depth_count = lax.axis_size("depth")
    phi_count = lax.axis_size("phi")
    owners = depth_count * phi_count
    slots = max(2, 2 * block_count // owners)
    owner_ids = owner[:, 0]
    onehot = (owner_ids[:, None] == jnp.arange(owners, dtype=jnp.int32)[None, :]).astype(jnp.int32)
    earlier = jnp.cumsum(onehot, axis=0) - onehot
    slot_index = jnp.sum(earlier * onehot, axis=1)
    position = owner_ids * slots + slot_index
    id_row = jnp.broadcast_to(
        (col_local + 1).astype(jnp.bfloat16)[:, None, None], (block_count, 1, cell_size)
    )
    payload = jnp.concatenate([partial_value, id_row], axis=1)
    placement = (
        position[None, :] == jnp.arange(owners * slots, dtype=jnp.int32)[:, None]
    ).astype(jnp.bfloat16)
    buffer = jnp.einsum(
        "sn,nck->sck", placement, payload, preferred_element_type=jnp.float32
    ).astype(jnp.bfloat16)
    received = lax.all_to_all(
        buffer.reshape(owners, slots, channels + 1, cell_size),
        ("depth", "phi"),
        split_axis=0,
        concat_axis=0,
        tiled=True,
    ).reshape(owners * slots, channels + 1, cell_size)
    got_cells = received[:, channels, 0].astype(jnp.int32)
    selector = (
        got_cells[None, :] == jnp.arange(1, CB_DEV + 1, dtype=jnp.int32)[:, None]
    ).astype(jnp.bfloat16)
    cell_grad = jnp.einsum(
        "ts,sck->tck", selector, received[:, :channels], preferred_element_type=jnp.float32
    )
    return cell_grad


def solution(mesh):
    return jax.shard_map(
        body,
        mesh=mesh,
        in_specs=(
            P("depth", "phi", None, None),
            P("depth", "phi", None, None),
            P(),
            P(),
            P(("depth", "phi"), None, None),
            P(("depth", "phi")),
            P(("depth", "phi"), None),
            P(("depth", "phi")),
        ),
        out_specs=P(("depth", "phi"), None, None),
        check_vma=False,
    )
```

```python
import functools

import jax
import jax.numpy as jnp
from jax import lax
from jax.experimental import pallas as pl
from jax.experimental.pallas import tpu as pltpu
from jax.sharding import PartitionSpec as P

CB_DEV = 12
TZ = 16


def halo_pieces(block):
    nq = lax.axis_size("phi")
    nd = lax.axis_size("depth")
    phi_fwd = [(q, (q + 1) % nq) for q in range(nq)]
    phi_bwd = [(t, s) for s, t in phi_fwd]
    dep_fwd = [(d, d + 1) for d in range(nd - 1)]
    dep_bwd = [(t, s) for s, t in dep_fwd]
    low_phi = lax.ppermute(block[:, -1:], "phi", phi_fwd)
    high_phi = lax.ppermute(block[:, :1], "phi", phi_bwd)
    first = jnp.concatenate([low_phi[:1], block[:1], high_phi[:1]], axis=1)
    last = jnp.concatenate([low_phi[-1:], block[-1:], high_phi[-1:]], axis=1)
    top = lax.ppermute(last, "depth", dep_fwd)
    bottom = lax.ppermute(first, "depth", dep_bwd)
    return block, low_phi, high_phi, top, bottom


def shifted(tile, c):
    if c == 0:
        return tile
    t = tile.astype(jnp.float32)
    e = t.shape[1]
    lane = lax.broadcasted_iota(jnp.int32, t.shape, 1)
    if c == 1:
        r = pltpu.roll(t, 1, 1)
        r = jnp.where(lane == 0, 0.0, r)
    else:
        r = pltpu.roll(t, e - 1, 1)
        r = jnp.where(lane == e - 1, 0.0, r)
    return r.astype(tile.dtype)


def conv_kernel(x_ref, lo_ref, hi_ref, top_ref, bot_ref, w_ref, side_ref, o_ref, y_ref,
                *, tz, pd, ch, mode):
    step = pl.program_id(0)
    eta = x_ref.shape[3]
    last_row = x_ref.shape[0] + 1

    def store(zin, q, tile):
        for c in (-1, 0, 1):
            sh = shifted(tile, c)
            for p in range(pd):
                b = p + 1 - q
                if -1 <= b <= 1:
                    y_ref[zin, b + 1, pl.ds((c + 1) * ch, ch), pl.ds(p * eta, eta)] = sh

    def build_end(zin, row_ref):
        for q in range(pd + 2):
            store(zin, q, row_ref[0, q])

    def build(zin):
        for q in range(pd + 2):
            if q == 0:
                tile = lo_ref[zin - 1, 0]
            elif q == pd + 1:
                tile = hi_ref[zin - 1, 0]
            else:
                tile = x_ref[zin - 1, q - 1]
            store(zin, q, tile)

    @pl.when(step == 0)
    def _():
        build_end(0, top_ref)
        build(1)

    def build_body(k, carry):
        zin = step * tz + 2 + k

        @pl.when(zin < last_row)
        def _():
            build(zin)

        @pl.when(zin == last_row)
        def _():
            build_end(last_row, bot_ref)

        return carry

    lax.fori_loop(0, tz, build_body, 0)

    def body(zz, carry):
        z = step * tz + zz
        rhs = y_ref[pl.ds(z, 3)].reshape(9 * 3 * ch, pd * eta)
        acc = jnp.dot(w_ref[...], rhs, preferred_element_type=jnp.float32)
        for p in range(pd):
            part = acc[:, p * eta:(p + 1) * eta]
            side = side_ref[zz, p].astype(jnp.float32)
            if mode == "hidden":
                sig = jax.nn.sigmoid(side)
                val = part * sig * (1.0 + side * (1.0 - sig))
            else:
                val = part + side
            o_ref[zz, p] = val.astype(o_ref.dtype)
        return carry

    lax.fori_loop(0, tz, body, 0)


def conv_call(pieces, weight, side, mode):
    field, low, high, top, bottom = pieces
    depth_len, pd, ch, eta = field.shape
    zp = depth_len + 2
    wfull = jnp.transpose(jnp.flip(weight, 0), (3, 0, 1, 2, 4)).reshape(ch, 27 * ch)

    def whole(a):
        return pl.BlockSpec(a.shape, lambda i: (0,) * a.ndim, pipeline_mode=pl.Buffered(1))

    return pl.pallas_call(
        functools.partial(conv_kernel, tz=TZ, pd=pd, ch=ch, mode=mode),
        grid=(depth_len // TZ,),
        in_specs=[
            whole(field), whole(low), whole(high), whole(top), whole(bottom), whole(wfull),
            pl.BlockSpec((TZ, pd, ch, eta), lambda i: (i, 0, 0, 0)),
        ],
        out_specs=pl.BlockSpec((TZ, pd, ch, eta), lambda i: (i, 0, 0, 0)),
        out_shape=jax.ShapeDtypeStruct((depth_len, pd, ch, eta), jnp.bfloat16),
        scratch_shapes=[pltpu.VMEM((zp, 3, 3 * ch, pd * eta), jnp.bfloat16)],
        compiler_params=pltpu.CompilerParams(vmem_limit_bytes=60 * 1024 * 1024),
    )(field, low, high, top, bottom, wfull, side)


def body(grad_out, pre_act, w_first, w_second, map_blocks, row_block, owner, col_local):
    hidden_grad = conv_call(halo_pieces(grad_out), w_second, pre_act, "hidden")
    grid_grad = conv_call(halo_pieces(hidden_grad), w_first, grad_out, "grid")
    channels = grid_grad.shape[2]
    eta_len = grid_grad.shape[3]
    block_count = map_blocks.shape[0]
    cell_size = map_blocks.shape[2]
    voxel_rows = grid_grad.reshape(grid_grad.shape[0] * grid_grad.shape[1], channels, eta_len)
    picked = voxel_rows[row_block]
    partial_value = jnp.einsum(
        "nce,nek->nck", picked, map_blocks, preferred_element_type=jnp.float32
    ).astype(jnp.bfloat16)
    depth_count = lax.axis_size("depth")
    phi_count = lax.axis_size("phi")
    owners = depth_count * phi_count
    slots = max(2, 2 * block_count // owners)
    owner_ids = owner[:, 0]
    onehot = (owner_ids[:, None] == jnp.arange(owners, dtype=jnp.int32)[None, :]).astype(jnp.int32)
    earlier = jnp.cumsum(onehot, axis=0) - onehot
    slot_index = jnp.sum(earlier * onehot, axis=1)
    position = owner_ids * slots + slot_index
    id_row = jnp.broadcast_to(
        (col_local + 1).astype(jnp.bfloat16)[:, None, None], (block_count, 1, cell_size)
    )
    payload = jnp.concatenate([partial_value, id_row], axis=1)
    placement = (
        position[None, :] == jnp.arange(owners * slots, dtype=jnp.int32)[:, None]
    ).astype(jnp.bfloat16)
    buffer = jnp.einsum(
        "sn,nck->sck", placement, payload, preferred_element_type=jnp.float32
    ).astype(jnp.bfloat16)
    received = lax.all_to_all(
        buffer.reshape(owners, slots, channels + 1, cell_size),
        ("depth", "phi"),
        split_axis=0,
        concat_axis=0,
        tiled=True,
    ).reshape(owners * slots, channels + 1, cell_size)
    got_cells = received[:, channels, 0].astype(jnp.int32)
    selector = (
        got_cells[None, :] == jnp.arange(1, CB_DEV + 1, dtype=jnp.int32)[:, None]
    ).astype(jnp.bfloat16)
    cell_grad = jnp.einsum(
        "ts,sck->tck", selector, received[:, :channels], preferred_element_type=jnp.float32
    )
    return cell_grad


def solution(mesh):
    return jax.shard_map(
        body,
        mesh=mesh,
        in_specs=(
            P("depth", "phi", None, None),
            P("depth", "phi", None, None),
            P(),
            P(),
            P(("depth", "phi"), None, None),
            P(("depth", "phi")),
            P(("depth", "phi"), None),
            P(("depth", "phi")),
        ),
        out_specs=P(("depth", "phi"), None, None),
        check_vma=False,
    )
```

```python
import functools

import jax
import jax.numpy as jnp
from jax import lax
from jax.experimental import pallas as pl
from jax.experimental.pallas import tpu as pltpu
from jax.sharding import PartitionSpec as P

CB_DEV = 12
TZ = 16


def halo_pieces(block):
    nq = lax.axis_size("phi")
    nd = lax.axis_size("depth")
    phi_fwd = [(q, (q + 1) % nq) for q in range(nq)]
    phi_bwd = [(t, s) for s, t in phi_fwd]
    dep_fwd = [(d, d + 1) for d in range(nd - 1)]
    dep_bwd = [(t, s) for s, t in dep_fwd]
    low_phi = lax.ppermute(block[:, -1:], "phi", phi_fwd)
    high_phi = lax.ppermute(block[:, :1], "phi", phi_bwd)
    first = jnp.concatenate([low_phi[:1], block[:1], high_phi[:1]], axis=1)
    last = jnp.concatenate([low_phi[-1:], block[-1:], high_phi[-1:]], axis=1)
    top = lax.ppermute(last, "depth", dep_fwd)
    bottom = lax.ppermute(first, "depth", dep_bwd)
    return block, low_phi, high_phi, top, bottom


def shifted(tile, c):
    if c == 0:
        return tile
    t = tile.astype(jnp.float32)
    e = t.shape[1]
    lane = lax.broadcasted_iota(jnp.int32, t.shape, 1)
    if c == 1:
        r = pltpu.roll(t, 1, 1)
        r = jnp.where(lane == 0, 0.0, r)
    else:
        r = pltpu.roll(t, e - 1, 1)
        r = jnp.where(lane == e - 1, 0.0, r)
    return r.astype(tile.dtype)


def conv_kernel(x_ref, lo_ref, hi_ref, top_ref, bot_ref, w_ref, side_ref, o_ref, y_ref,
                *, tz, pd, ch, mode):
    step = pl.program_id(0)
    eta = x_ref.shape[3]
    last_row = x_ref.shape[0] + 1

    def store(zin, q, tile):
        for c in (-1, 0, 1):
            sh = shifted(tile, c)
            for p in range(pd):
                b = p + 1 - q
                if -1 <= b <= 1:
                    y_ref[zin, b + 1, pl.ds((c + 1) * ch, ch), pl.ds(p * eta, eta)] = sh

    def build_end(zin, row_ref):
        for q in range(pd + 2):
            store(zin, q, row_ref[0, q])

    def build(zin):
        for q in range(pd + 2):
            if q == 0:
                tile = lo_ref[zin - 1, 0]
            elif q == pd + 1:
                tile = hi_ref[zin - 1, 0]
            else:
                tile = x_ref[zin - 1, q - 1]
            store(zin, q, tile)

    @pl.when(step == 0)
    def _():
        build_end(0, top_ref)
        build(1)

    def build_body(k, carry):
        zin = step * tz + 2 + k

        @pl.when(zin < last_row)
        def _():
            build(zin)

        @pl.when(zin == last_row)
        def _():
            build_end(last_row, bot_ref)

        return carry

    lax.fori_loop(0, tz, build_body, 0)

    def body(zz, carry):
        z = step * tz + zz
        rhs = y_ref[pl.ds(z, 3)].reshape(9 * 3 * ch, pd * eta)
        acc = jnp.dot(w_ref[...], rhs, preferred_element_type=jnp.float32)
        for p in range(pd):
            part = acc[:, p * eta:(p + 1) * eta]
            side = side_ref[zz, p].astype(jnp.float32)
            if mode == "hidden":
                sig = jax.nn.sigmoid(side)
                val = part * sig * (1.0 + side * (1.0 - sig))
            else:
                val = part + side
            o_ref[zz, p] = val.astype(o_ref.dtype)
        return carry

    lax.fori_loop(0, tz, body, 0)


def conv_call(pieces, weight, side, mode):
    field, low, high, top, bottom = pieces
    depth_len, pd, ch, eta = field.shape
    zp = depth_len + 2
    wfull = jnp.transpose(jnp.flip(weight, 0), (3, 0, 1, 2, 4)).reshape(ch, 27 * ch)

    def whole(a):
        return pl.BlockSpec(a.shape, lambda i: (0,) * a.ndim, pipeline_mode=pl.Buffered(1))

    return pl.pallas_call(
        functools.partial(conv_kernel, tz=TZ, pd=pd, ch=ch, mode=mode),
        grid=(depth_len // TZ,),
        in_specs=[
            whole(field), whole(low), whole(high), whole(top), whole(bottom), whole(wfull),
            pl.BlockSpec((TZ, pd, ch, eta), lambda i: (i, 0, 0, 0)),
        ],
        out_specs=pl.BlockSpec((TZ, pd, ch, eta), lambda i: (i, 0, 0, 0)),
        out_shape=jax.ShapeDtypeStruct((depth_len, pd, ch, eta), jnp.bfloat16),
        scratch_shapes=[pltpu.VMEM((zp, 3, 3 * ch, pd * eta), jnp.bfloat16)],
        compiler_params=pltpu.CompilerParams(vmem_limit_bytes=60 * 1024 * 1024),
    )(field, low, high, top, bottom, wfull, side)


def body(grad_out, pre_act, w_first, w_second, map_blocks, row_block, owner, col_local):
    hidden_grad = conv_call(halo_pieces(grad_out), w_second, pre_act, "hidden")
    grid_grad = conv_call(halo_pieces(hidden_grad), w_first, grad_out, "grid")
    channels = grid_grad.shape[2]
    eta_len = grid_grad.shape[3]
    block_count = map_blocks.shape[0]
    cell_size = map_blocks.shape[2]
    voxel_rows = grid_grad.reshape(grid_grad.shape[0] * grid_grad.shape[1], channels, eta_len)
    picked = voxel_rows[row_block]
    partial_value = jnp.einsum(
        "nce,nek->nck", picked, map_blocks, preferred_element_type=jnp.float32
    ).astype(jnp.bfloat16)
    depth_count = lax.axis_size("depth")
    phi_count = lax.axis_size("phi")
    owners = depth_count * phi_count
    slots = max(2, 2 * block_count // owners)
    owner_ids = owner[:, 0]
    onehot = (owner_ids[:, None] == jnp.arange(owners, dtype=jnp.int32)[None, :]).astype(jnp.int32)
    earlier = jnp.cumsum(onehot, axis=0) - onehot
    slot_index = jnp.sum(earlier * onehot, axis=1)
    position = owner_ids * slots + slot_index
    id_row = jnp.broadcast_to(
        (col_local + 1).astype(jnp.bfloat16)[:, None, None], (block_count, 1, cell_size)
    )
    payload = jnp.concatenate([partial_value, id_row], axis=1)
    placement = (
        position[None, :] == jnp.arange(owners * slots, dtype=jnp.int32)[:, None]
    ).astype(jnp.bfloat16)
    buffer = jnp.einsum(
        "sn,nck->sck", placement, payload, preferred_element_type=jnp.float32
    ).astype(jnp.bfloat16)
    staged = lax.all_to_all(
        buffer.reshape(depth_count, phi_count, slots, channels + 1, cell_size),
        "phi", split_axis=1, concat_axis=1, tiled=True,
    )
    received = lax.all_to_all(
        staged, "depth", split_axis=0, concat_axis=0, tiled=True,
    ).reshape(owners * slots, channels + 1, cell_size)
    got_cells = received[:, channels, 0].astype(jnp.int32)
    selector = (
        got_cells[None, :] == jnp.arange(1, CB_DEV + 1, dtype=jnp.int32)[:, None]
    ).astype(jnp.bfloat16)
    cell_grad = jnp.einsum(
        "ts,sck->tck", selector, received[:, :channels], preferred_element_type=jnp.float32
    )
    return cell_grad


def solution(mesh):
    return jax.shard_map(
        body,
        mesh=mesh,
        in_specs=(
            P("depth", "phi", None, None),
            P("depth", "phi", None, None),
            P(),
            P(),
            P(("depth", "phi"), None, None),
            P(("depth", "phi")),
            P(("depth", "phi"), None),
            P(("depth", "phi")),
        ),
        out_specs=P(("depth", "phi"), None, None),
        check_vma=False,
    )
```

```python
import functools

import jax
import jax.numpy as jnp
from jax import lax
from jax.experimental import pallas as pl
from jax.experimental.pallas import tpu as pltpu
from jax.sharding import PartitionSpec as P

CB_DEV = 12
TZ = 16


def halo_pieces(block):
    nq = lax.axis_size("phi")
    nd = lax.axis_size("depth")
    phi_fwd = [(q, (q + 1) % nq) for q in range(nq)]
    phi_bwd = [(t, s) for s, t in phi_fwd]
    dep_fwd = [(d, d + 1) for d in range(nd - 1)]
    dep_bwd = [(t, s) for s, t in dep_fwd]
    low_phi = lax.ppermute(block[:, -1:], "phi", phi_fwd)
    high_phi = lax.ppermute(block[:, :1], "phi", phi_bwd)
    first = jnp.concatenate([low_phi[:1], block[:1], high_phi[:1]], axis=1)
    last = jnp.concatenate([low_phi[-1:], block[-1:], high_phi[-1:]], axis=1)
    top = lax.ppermute(last, "depth", dep_fwd)
    bottom = lax.ppermute(first, "depth", dep_bwd)
    return block, low_phi, high_phi, top, bottom


def shifted(tile, c):
    if c == 0:
        return tile
    t = tile.astype(jnp.float32)
    e = t.shape[1]
    lane = lax.broadcasted_iota(jnp.int32, t.shape, 1)
    if c == 1:
        r = pltpu.roll(t, 1, 1)
        r = jnp.where(lane == 0, 0.0, r)
    else:
        r = pltpu.roll(t, e - 1, 1)
        r = jnp.where(lane == e - 1, 0.0, r)
    return r.astype(tile.dtype)


def conv_kernel(x_ref, lo_ref, hi_ref, top_ref, bot_ref, w_ref, side_ref, o_ref, y_ref,
                *, tz, pd, ch, mode):
    step = pl.program_id(0)
    eta = x_ref.shape[3]
    last_row = x_ref.shape[0] + 1

    def store(zin, q, tile):
        for c in (-1, 0, 1):
            sh = shifted(tile, c)
            for p in range(pd):
                b = p + 1 - q
                if -1 <= b <= 1:
                    y_ref[zin, b + 1, pl.ds((c + 1) * ch, ch), pl.ds(p * eta, eta)] = sh

    def build_end(zin, row_ref):
        for q in range(pd + 2):
            store(zin, q, row_ref[0, q])

    def build(zin):
        for q in range(pd + 2):
            if q == 0:
                tile = lo_ref[zin - 1, 0]
            elif q == pd + 1:
                tile = hi_ref[zin - 1, 0]
            else:
                tile = x_ref[zin - 1, q - 1]
            store(zin, q, tile)

    @pl.when(step == 0)
    def _():
        build_end(0, top_ref)
        build(1)
        build(2)
        build_end(last_row, bot_ref)

    def body(zz, carry):
        z = step * tz + zz
        build(jnp.minimum(z + 3, last_row - 1))
        rhs = y_ref[pl.ds(z, 3)].reshape(9 * 3 * ch, pd * eta)
        acc = jnp.dot(w_ref[...], rhs, preferred_element_type=jnp.float32)
        for p in range(pd):
            part = acc[:, p * eta:(p + 1) * eta]
            side = side_ref[zz, p].astype(jnp.float32)
            if mode == "hidden":
                sig = jax.nn.sigmoid(side)
                val = part * sig * (1.0 + side * (1.0 - sig))
            else:
                val = part + side
            o_ref[zz, p] = val.astype(o_ref.dtype)
        return carry

    lax.fori_loop(0, tz, body, 0)


def conv_call(pieces, weight, side, mode):
    field, low, high, top, bottom = pieces
    depth_len, pd, ch, eta = field.shape
    zp = depth_len + 2
    wfull = jnp.transpose(jnp.flip(weight, 0), (3, 0, 1, 2, 4)).reshape(ch, 27 * ch)

    def whole(a):
        return pl.BlockSpec(a.shape, lambda i: (0,) * a.ndim, pipeline_mode=pl.Buffered(1))

    return pl.pallas_call(
        functools.partial(conv_kernel, tz=TZ, pd=pd, ch=ch, mode=mode),
        grid=(depth_len // TZ,),
        in_specs=[
            whole(field), whole(low), whole(high), whole(top), whole(bottom), whole(wfull),
            pl.BlockSpec((TZ, pd, ch, eta), lambda i: (i, 0, 0, 0)),
        ],
        out_specs=pl.BlockSpec((TZ, pd, ch, eta), lambda i: (i, 0, 0, 0)),
        out_shape=jax.ShapeDtypeStruct((depth_len, pd, ch, eta), jnp.bfloat16),
        scratch_shapes=[pltpu.VMEM((zp, 3, 3 * ch, pd * eta), jnp.bfloat16)],
        compiler_params=pltpu.CompilerParams(vmem_limit_bytes=60 * 1024 * 1024),
    )(field, low, high, top, bottom, wfull, side)


def body(grad_out, pre_act, w_first, w_second, map_blocks, row_block, owner, col_local):
    hidden_grad = conv_call(halo_pieces(grad_out), w_second, pre_act, "hidden")
    grid_grad = conv_call(halo_pieces(hidden_grad), w_first, grad_out, "grid")
    channels = grid_grad.shape[2]
    eta_len = grid_grad.shape[3]
    block_count = map_blocks.shape[0]
    cell_size = map_blocks.shape[2]
    voxel_rows = grid_grad.reshape(grid_grad.shape[0] * grid_grad.shape[1], channels, eta_len)
    picked = voxel_rows[row_block]
    partial_value = jnp.einsum(
        "nce,nek->nck", picked, map_blocks, preferred_element_type=jnp.float32
    ).astype(jnp.bfloat16)
    depth_count = lax.axis_size("depth")
    phi_count = lax.axis_size("phi")
    owners = depth_count * phi_count
    slots = max(2, 2 * block_count // owners)
    owner_ids = owner[:, 0]
    onehot = (owner_ids[:, None] == jnp.arange(owners, dtype=jnp.int32)[None, :]).astype(jnp.int32)
    earlier = jnp.cumsum(onehot, axis=0) - onehot
    slot_index = jnp.sum(earlier * onehot, axis=1)
    position = owner_ids * slots + slot_index
    id_row = jnp.broadcast_to(
        (col_local + 1).astype(jnp.bfloat16)[:, None, None], (block_count, 1, cell_size)
    )
    payload = jnp.concatenate([partial_value, id_row], axis=1)
    placement = (
        position[None, :] == jnp.arange(owners * slots, dtype=jnp.int32)[:, None]
    ).astype(jnp.bfloat16)
    buffer = jnp.einsum(
        "sn,nck->sck", placement, payload, preferred_element_type=jnp.float32
    ).astype(jnp.bfloat16)
    received = lax.all_to_all(
        buffer.reshape(owners, slots, channels + 1, cell_size),
        ("depth", "phi"),
        split_axis=0,
        concat_axis=0,
        tiled=True,
    ).reshape(owners * slots, channels + 1, cell_size)
    got_cells = received[:, channels, 0].astype(jnp.int32)
    selector = (
        got_cells[None, :] == jnp.arange(1, CB_DEV + 1, dtype=jnp.int32)[:, None]
    ).astype(jnp.bfloat16)
    cell_grad = jnp.einsum(
        "ts,sck->tck", selector, received[:, :channels], preferred_element_type=jnp.float32
    )
    return cell_grad


def solution(mesh):
    return jax.shard_map(
        body,
        mesh=mesh,
        in_specs=(
            P("depth", "phi", None, None),
            P("depth", "phi", None, None),
            P(),
            P(),
            P(("depth", "phi"), None, None),
            P(("depth", "phi")),
            P(("depth", "phi"), None),
            P(("depth", "phi")),
        ),
        out_specs=P(("depth", "phi"), None, None),
        check_vma=False,
    )
```

```python
import functools

import jax
import jax.numpy as jnp
from jax import lax
from jax.experimental import pallas as pl
from jax.experimental.pallas import tpu as pltpu
from jax.sharding import PartitionSpec as P

CB_DEV = 12
TZ = 16


def halo_pieces(block):
    nq = lax.axis_size("phi")
    nd = lax.axis_size("depth")
    phi_fwd = [(q, (q + 1) % nq) for q in range(nq)]
    phi_bwd = [(t, s) for s, t in phi_fwd]
    dep_fwd = [(d, d + 1) for d in range(nd - 1)]
    dep_bwd = [(t, s) for s, t in dep_fwd]
    low_phi = lax.ppermute(block[:, -1:], "phi", phi_fwd)
    high_phi = lax.ppermute(block[:, :1], "phi", phi_bwd)
    first = jnp.concatenate([low_phi[:1], block[:1], high_phi[:1]], axis=1)
    last = jnp.concatenate([low_phi[-1:], block[-1:], high_phi[-1:]], axis=1)
    top = lax.ppermute(last, "depth", dep_fwd)
    bottom = lax.ppermute(first, "depth", dep_bwd)
    return block, low_phi, high_phi, top, bottom


def shifted(tile, c):
    if c == 0:
        return tile
    t = tile.astype(jnp.float32)
    e = t.shape[1]
    lane = lax.broadcasted_iota(jnp.int32, t.shape, 1)
    if c == 1:
        r = pltpu.roll(t, 1, 1)
        r = jnp.where(lane == 0, 0.0, r)
    else:
        r = pltpu.roll(t, e - 1, 1)
        r = jnp.where(lane == e - 1, 0.0, r)
    return r.astype(tile.dtype)


def conv_kernel(x_ref, lo_ref, hi_ref, top_ref, bot_ref, w_ref, side_ref, o_ref, y_ref,
                *, tz, pd, ch, mode):
    step = pl.program_id(0)
    eta = x_ref.shape[3]
    last_row = x_ref.shape[0] + 1

    def store(zin, q, tile):
        for c in (-1, 0, 1):
            sh = shifted(tile, c)
            for p in range(pd):
                b = p + 1 - q
                if -1 <= b <= 1:
                    y_ref[zin, b + 1, pl.ds((c + 1) * ch, ch), pl.ds(p * eta, eta)] = sh

    def build_end(zin, row_ref):
        for q in range(pd + 2):
            store(zin, q, row_ref[0, q])

    def build(zin):
        for q in range(pd + 2):
            if q == 0:
                tile = lo_ref[zin - 1, 0]
            elif q == pd + 1:
                tile = hi_ref[zin - 1, 0]
            else:
                tile = x_ref[zin - 1, q - 1]
            store(zin, q, tile)

    @pl.when(step == 0)
    def _():
        build_end(0, top_ref)
        build(1)
        build(2)
        build_end(last_row, bot_ref)

    def body(zz, carry):
        z = step * tz + zz
        build(jnp.minimum(z + 3, last_row - 1))
        rhs = y_ref[pl.ds(z, 3)].reshape(9 * 3 * ch, pd * eta)
        acc = jnp.dot(w_ref[...], rhs, preferred_element_type=jnp.float32)
        for p in range(pd):
            part = acc[:, p * eta:(p + 1) * eta]
            side = side_ref[zz, p].astype(jnp.float32)
            if mode == "hidden":
                sig = jax.nn.sigmoid(side)
                val = part * sig * (1.0 + side * (1.0 - sig))
            else:
                val = part + side
            o_ref[zz, p] = val.astype(o_ref.dtype)
        return carry

    lax.fori_loop(0, tz, body, 0, unroll=True)


def conv_call(pieces, weight, side, mode):
    field, low, high, top, bottom = pieces
    depth_len, pd, ch, eta = field.shape
    zp = depth_len + 2
    wfull = jnp.transpose(jnp.flip(weight, 0), (3, 0, 1, 2, 4)).reshape(ch, 27 * ch)

    def whole(a):
        return pl.BlockSpec(a.shape, lambda i: (0,) * a.ndim, pipeline_mode=pl.Buffered(1))

    return pl.pallas_call(
        functools.partial(conv_kernel, tz=TZ, pd=pd, ch=ch, mode=mode),
        grid=(depth_len // TZ,),
        in_specs=[
            whole(field), whole(low), whole(high), whole(top), whole(bottom), whole(wfull),
            pl.BlockSpec((TZ, pd, ch, eta), lambda i: (i, 0, 0, 0)),
        ],
        out_specs=pl.BlockSpec((TZ, pd, ch, eta), lambda i: (i, 0, 0, 0)),
        out_shape=jax.ShapeDtypeStruct((depth_len, pd, ch, eta), jnp.bfloat16),
        scratch_shapes=[pltpu.VMEM((zp, 3, 3 * ch, pd * eta), jnp.bfloat16)],
        compiler_params=pltpu.CompilerParams(vmem_limit_bytes=60 * 1024 * 1024),
    )(field, low, high, top, bottom, wfull, side)


def body(grad_out, pre_act, w_first, w_second, map_blocks, row_block, owner, col_local):
    hidden_grad = conv_call(halo_pieces(grad_out), w_second, pre_act, "hidden")
    grid_grad = conv_call(halo_pieces(hidden_grad), w_first, grad_out, "grid")
    channels = grid_grad.shape[2]
    eta_len = grid_grad.shape[3]
    block_count = map_blocks.shape[0]
    cell_size = map_blocks.shape[2]
    voxel_rows = grid_grad.reshape(grid_grad.shape[0] * grid_grad.shape[1], channels, eta_len)
    picked = voxel_rows[row_block]
    partial_value = jnp.einsum(
        "nce,nek->nck", picked, map_blocks, preferred_element_type=jnp.float32
    ).astype(jnp.bfloat16)
    depth_count = lax.axis_size("depth")
    phi_count = lax.axis_size("phi")
    owners = depth_count * phi_count
    slots = max(2, 2 * block_count // owners)
    owner_ids = owner[:, 0]
    onehot = (owner_ids[:, None] == jnp.arange(owners, dtype=jnp.int32)[None, :]).astype(jnp.int32)
    earlier = jnp.cumsum(onehot, axis=0) - onehot
    slot_index = jnp.sum(earlier * onehot, axis=1)
    position = owner_ids * slots + slot_index
    id_row = jnp.broadcast_to(
        (col_local + 1).astype(jnp.bfloat16)[:, None, None], (block_count, 1, cell_size)
    )
    payload = jnp.concatenate([partial_value, id_row], axis=1)
    placement = (
        position[None, :] == jnp.arange(owners * slots, dtype=jnp.int32)[:, None]
    ).astype(jnp.bfloat16)
    buffer = jnp.einsum(
        "sn,nck->sck", placement, payload, preferred_element_type=jnp.float32
    ).astype(jnp.bfloat16)
    received = lax.all_to_all(
        buffer.reshape(owners, slots, channels + 1, cell_size),
        ("depth", "phi"),
        split_axis=0,
        concat_axis=0,
        tiled=True,
    ).reshape(owners * slots, channels + 1, cell_size)
    got_cells = received[:, channels, 0].astype(jnp.int32)
    selector = (
        got_cells[None, :] == jnp.arange(1, CB_DEV + 1, dtype=jnp.int32)[:, None]
    ).astype(jnp.bfloat16)
    cell_grad = jnp.einsum(
        "ts,sck->tck", selector, received[:, :channels], preferred_element_type=jnp.float32
    )
    return cell_grad


def solution(mesh):
    return jax.shard_map(
        body,
        mesh=mesh,
        in_specs=(
            P("depth", "phi", None, None),
            P("depth", "phi", None, None),
            P(),
            P(),
            P(("depth", "phi"), None, None),
            P(("depth", "phi")),
            P(("depth", "phi"), None),
            P(("depth", "phi")),
        ),
        out_specs=P(("depth", "phi"), None, None),
        check_vma=False,
    )
```

```python
import functools

import jax
import jax.numpy as jnp
from jax import lax
from jax.experimental import pallas as pl
from jax.experimental.pallas import tpu as pltpu
from jax.sharding import PartitionSpec as P

CB_DEV = 12
TZ = 28


def halo_pieces(block):
    nq = lax.axis_size("phi")
    nd = lax.axis_size("depth")
    phi_fwd = [(q, (q + 1) % nq) for q in range(nq)]
    phi_bwd = [(t, s) for s, t in phi_fwd]
    dep_fwd = [(d, d + 1) for d in range(nd - 1)]
    dep_bwd = [(t, s) for s, t in dep_fwd]
    low_phi = lax.ppermute(block[:, -1:], "phi", phi_fwd)
    high_phi = lax.ppermute(block[:, :1], "phi", phi_bwd)
    first = jnp.concatenate([low_phi[:1], block[:1], high_phi[:1]], axis=1)
    last = jnp.concatenate([low_phi[-1:], block[-1:], high_phi[-1:]], axis=1)
    top = lax.ppermute(last, "depth", dep_fwd)
    bottom = lax.ppermute(first, "depth", dep_bwd)
    return block, low_phi, high_phi, top, bottom


def shifted(tile, c):
    if c == 0:
        return tile
    t = tile.astype(jnp.float32)
    e = t.shape[1]
    lane = lax.broadcasted_iota(jnp.int32, t.shape, 1)
    if c == 1:
        r = pltpu.roll(t, 1, 1)
        r = jnp.where(lane == 0, 0.0, r)
    else:
        r = pltpu.roll(t, e - 1, 1)
        r = jnp.where(lane == e - 1, 0.0, r)
    return r.astype(tile.dtype)


def conv_kernel(x_ref, lo_ref, hi_ref, top_ref, bot_ref, w_ref, side_ref, o_ref, y_ref,
                *, tz, pd, ch, mode):
    step = pl.program_id(0)
    eta = x_ref.shape[3]
    last_row = x_ref.shape[0] + 1

    def store(zin, q, tile):
        for c in (-1, 0, 1):
            sh = shifted(tile, c)
            for p in range(pd):
                b = p + 1 - q
                if -1 <= b <= 1:
                    y_ref[zin, b + 1, pl.ds((c + 1) * ch, ch), pl.ds(p * eta, eta)] = sh

    def build_end(zin, row_ref):
        for q in range(pd + 2):
            store(zin, q, row_ref[0, q])

    def build(zin):
        for q in range(pd + 2):
            if q == 0:
                tile = lo_ref[zin - 1, 0]
            elif q == pd + 1:
                tile = hi_ref[zin - 1, 0]
            else:
                tile = x_ref[zin - 1, q - 1]
            store(zin, q, tile)

    @pl.when(step == 0)
    def _():
        build_end(0, top_ref)
        build(1)
        build(2)
        build_end(last_row, bot_ref)

    def body(zz, carry):
        z = step * tz + zz
        build(jnp.minimum(z + 3, last_row - 1))
        rhs = y_ref[pl.ds(z, 3)].reshape(9 * 3 * ch, pd * eta)
        acc = jnp.dot(w_ref[...], rhs, preferred_element_type=jnp.float32)
        for p in range(pd):
            part = acc[:, p * eta:(p + 1) * eta]
            side = side_ref[zz, p].astype(jnp.float32)
            if mode == "hidden":
                sig = jax.nn.sigmoid(side)
                val = part * sig * (1.0 + side * (1.0 - sig))
            else:
                val = part + side
            o_ref[zz, p] = val.astype(o_ref.dtype)
        return carry

    lax.fori_loop(0, tz, body, 0, unroll=True)


def conv_call(pieces, weight, side, mode):
    field, low, high, top, bottom = pieces
    depth_len, pd, ch, eta = field.shape
    zp = depth_len + 2
    wfull = jnp.transpose(jnp.flip(weight, 0), (3, 0, 1, 2, 4)).reshape(ch, 27 * ch)

    def whole(a):
        return pl.BlockSpec(a.shape, lambda i: (0,) * a.ndim, pipeline_mode=pl.Buffered(1))

    return pl.pallas_call(
        functools.partial(conv_kernel, tz=TZ, pd=pd, ch=ch, mode=mode),
        grid=(depth_len // TZ,),
        in_specs=[
            whole(field), whole(low), whole(high), whole(top), whole(bottom), whole(wfull),
            pl.BlockSpec((TZ, pd, ch, eta), lambda i: (i, 0, 0, 0)),
        ],
        out_specs=pl.BlockSpec((TZ, pd, ch, eta), lambda i: (i, 0, 0, 0)),
        out_shape=jax.ShapeDtypeStruct((depth_len, pd, ch, eta), jnp.bfloat16),
        scratch_shapes=[pltpu.VMEM((zp, 3, 3 * ch, pd * eta), jnp.bfloat16)],
        compiler_params=pltpu.CompilerParams(vmem_limit_bytes=60 * 1024 * 1024),
    )(field, low, high, top, bottom, wfull, side)


def body(grad_out, pre_act, w_first, w_second, map_blocks, row_block, owner, col_local):
    hidden_grad = conv_call(halo_pieces(grad_out), w_second, pre_act, "hidden")
    grid_grad = conv_call(halo_pieces(hidden_grad), w_first, grad_out, "grid")
    channels = grid_grad.shape[2]
    eta_len = grid_grad.shape[3]
    block_count = map_blocks.shape[0]
    cell_size = map_blocks.shape[2]
    voxel_rows = grid_grad.reshape(grid_grad.shape[0] * grid_grad.shape[1], channels, eta_len)
    picked = voxel_rows[row_block]
    partial_value = jnp.einsum(
        "nce,nek->nck", picked, map_blocks, preferred_element_type=jnp.float32
    ).astype(jnp.bfloat16)
    depth_count = lax.axis_size("depth")
    phi_count = lax.axis_size("phi")
    owners = depth_count * phi_count
    slots = max(2, 2 * block_count // owners)
    owner_ids = owner[:, 0]
    onehot = (owner_ids[:, None] == jnp.arange(owners, dtype=jnp.int32)[None, :]).astype(jnp.int32)
    earlier = jnp.cumsum(onehot, axis=0) - onehot
    slot_index = jnp.sum(earlier * onehot, axis=1)
    position = owner_ids * slots + slot_index
    id_row = jnp.broadcast_to(
        (col_local + 1).astype(jnp.bfloat16)[:, None, None], (block_count, 1, cell_size)
    )
    payload = jnp.concatenate([partial_value, id_row], axis=1)
    placement = (
        position[None, :] == jnp.arange(owners * slots, dtype=jnp.int32)[:, None]
    ).astype(jnp.bfloat16)
    buffer = jnp.einsum(
        "sn,nck->sck", placement, payload, preferred_element_type=jnp.float32
    ).astype(jnp.bfloat16)
    received = lax.all_to_all(
        buffer.reshape(owners, slots, channels + 1, cell_size),
        ("depth", "phi"),
        split_axis=0,
        concat_axis=0,
        tiled=True,
    ).reshape(owners * slots, channels + 1, cell_size)
    got_cells = received[:, channels, 0].astype(jnp.int32)
    selector = (
        got_cells[None, :] == jnp.arange(1, CB_DEV + 1, dtype=jnp.int32)[:, None]
    ).astype(jnp.bfloat16)
    cell_grad = jnp.einsum(
        "ts,sck->tck", selector, received[:, :channels], preferred_element_type=jnp.float32
    )
    return cell_grad


def solution(mesh):
    return jax.shard_map(
        body,
        mesh=mesh,
        in_specs=(
            P("depth", "phi", None, None),
            P("depth", "phi", None, None),
            P(),
            P(),
            P(("depth", "phi"), None, None),
            P(("depth", "phi")),
            P(("depth", "phi"), None),
            P(("depth", "phi")),
        ),
        out_specs=P(("depth", "phi"), None, None),
        check_vma=False,
    )
```
